32 devices in a mesh: ep: 16 (over z, y, core), dp: 2 (over x).
Axes of the slice: x: 2, y: 2, z: 4, core: 2. Of those that a mesh axis runs over, the one named last changes fastest.
Arguments:
- moe_rows: bfloat16 [1024, 3584], P(('dp', 'ep')), parts along dimension 0, may hold values from -6 to 6
- routes: int32 [1024, 4], P(('dp', 'ep')), parts along dimension 0, may hold values from 0 to 7, all different within a row; in each aligned block of 32 rows (0 to 31, 32 to 63, ...) at most 32 rows name the same one
- route_weights: float32 [1024, 4], P(('dp', 'ep')), parts along dimension 0, may hold values from 0.05 to 0.5
- w_gate: bfloat16 [16, 3584, 512], P('ep'), may hold values from -0.09375 to 0.09375
- w_up: bfloat16 [16, 3584, 512], P('ep'), may hold values from -0.09375 to 0.09375
- w_down: bfloat16 [16, 512, 3584], P('ep'), may hold values from -0.1875 to 0.1875
- queries: bfloat16 [128, 64, 576], P(('dp', 'ep')), parts along dimension 0, may hold values from -45 to 45
- latent_cache: bfloat16 [128, 128, 576], P(('dp', 'ep')), parts along dimension 0, may hold values from -6 to 6
- lengths: int32 [128], P(('dp', 'ep')), parts along dimension 0, may hold values from 2 to 128, as said below
Outputs:
- moe_out: bfloat16 [1024, 3584], P(('dp', 'ep')), parts along dimension 0
- attn_out: bfloat16 [128, 64, 512], P(('dp', 'ep')), parts along dimension 0
The draws below stay inside these ranges and needn't reach their ends.
There are 2 independent parts, one for each index of `dp`. The reference program is written for one: setup_inputs(seed, part) draws one part's arguments, and reference() takes and returns one part's arrays. A program takes and returns all parts, laid end to end along the dimension named above; an argument that names none is the same for every part. Nothing has to cross between parts.
Inputs may be any that keep to these rules, and one draw needn't show every extreme that they name: `routes`: each row names 4 different experts; in each aligned block of 32 rows (the rows of one device) no expert is named by more than 32 rows, a bound that some block reaches. `lengths`: some row of every part uses all 128 positions.
All inputs are finite; a program needn't handle non-finite values.
Results may differ from the reference program's by a relative error of at most 0.0085.
Values may be sent and summed in bfloat16 or wider, within the bound.
No kernel may reach another device: no remote copies, remote signals or barrier semaphores. Data moves between devices by JAX's collectives and lax.ppermute only.
A program may use at most 128 MiB of HBM per device.

```python
import math
import jax
import jax.numpy as jnp
import numpy as np
from jax import lax

D = 3584
FF = 1024
HEADS = 64
LATENT = 512
CTX = 128
TOP = 4
ROWS_DEV = 32
KV = 576
FF_HALF = 512
EXPERTS = 8
CAP = 32
ROWS = 512
ATT_ROWS = 64
N_EP = 16


def attention_draw(key):
    folded = jax.random.fold_in(key, 7)
    key_query, key_cache = jax.random.split(folded, 2)
    cached = jnp.clip(jax.random.normal(key_cache, (ATT_ROWS, CTX, KV), jnp.float32), -5.0, 5.0)
    asked = jnp.clip(jax.random.normal(key_query, (ATT_ROWS, HEADS, KV), jnp.float32), -5.0, 5.0)
    return (asked, cached)


def draw_queries(key, part):
    return attention_draw(key)[0].astype(jnp.bfloat16)


def draw_latent_cache(key, part):
    return attention_draw(key)[1].astype(jnp.bfloat16)


def draw_lengths(key, part):
    key_lengths, key_full = jax.random.split(jax.random.fold_in(key, 3))
    spans = jax.random.randint(key_lengths, (ATT_ROWS,), 2, CTX + 1)
    longest = jax.random.randint(key_full, (), 0, ATT_ROWS)
    return spans.at[longest].set(CTX).astype(jnp.int32)


def steps_of(key, shape, pieces, low, high):
    level, own = 1.0, jax.random.fold_in(key, 6)
    for axis_at, parts in pieces:
        steps = jnp.exp(jax.random.uniform(jax.random.fold_in(own, axis_at), (parts,), jnp.float32, low / len(pieces), high / len(pieces)))
        level = level * jnp.repeat(steps, shape[axis_at] // parts).reshape([-1 if axis == axis_at else 1 for axis in range(len(shape))])
    return level


def routed_block(rng, own, number, rows, number_of, top, limit, lean):
    order = jax.random.permutation(rng, number_of)
    packed, usual = load_shares(number_of, rows * top, limit, lean, True), load_shares(number_of, rows * top, limit, lean, False)
    places = jnp.arange(number_of)

    def named(tallies, rotation):
        used = int((tallies > 0).sum())
        fixed = max(1, used // 4)
        shifted = fixed + (places - fixed + rotation * (used - fixed)) % max(1, number_of - fixed)
        return jnp.zeros((number_of,), jnp.int32).at[order[jnp.where(places < fixed, places, shifted)]].set(jnp.asarray(tallies, jnp.int32))

    tallies = jnp.where(number % 4 == 0, named(packed, number // 4), named(usual, number - number // 4 - 1))
    mixed = jax.random.permutation(jax.random.fold_in(own, 3), number_of)
    giver, taker = mixed[0:number_of // 2 * 2:2], mixed[1:number_of // 2 * 2:2]
    slack = jnp.minimum(tallies[giver] - 1, limit - tallies[taker]) // 2
    slack = jnp.where((giver == order[0]) | (taker == order[0]) | (tallies[taker] == 0), 0, jnp.maximum(slack, 0))
    shifted = jax.random.randint(jax.random.fold_in(own, 4), (number_of // 2,), 0, 1 << 20) % (slack + 1)
    tallies = tallies.at[giver].add(-shifted).at[taker].add(shifted)
    items = jnp.searchsorted(jnp.cumsum(tallies), jnp.arange(rows * top), side="right").astype(jnp.int32)
    table = items.reshape(top, rows).T
    table = table[jax.random.permutation(jax.random.fold_in(own, 1), rows)]
    rotation = jax.random.randint(jax.random.fold_in(own, 2), (rows, 1), 0, top)
    return jnp.take_along_axis(table, (jnp.arange(top)[None, :] + rotation) % top, axis=1)


def load_shares(number_of, total, most, slope, full):
    weights = [(1 << 20) // math.isqrt(rank ** slope) + 1 for rank in range(1, number_of + 1)]
    largest = most if full else min(most, max(-(-total // number_of), total * weights[0] // sum(weights)))
    least = 1 if total - largest >= number_of - 1 else 0
    given, surplus = [largest] + [least] * (number_of - 1), total - largest - least * (number_of - 1)
    while surplus > 0:
        candidates = [i for i in range(1, number_of) if given[i] < largest] or [i for i in range(1, number_of) if given[i] < most]
        mass, budget = sum([weights[i] for i in candidates]), surplus
        for i in candidates:
            extra = min(most - given[i], max(1, budget * weights[i] // mass), surplus)
            given[i] = given[i] + extra
            surplus = surplus - extra
    return np.array(given)


def centred(key, shape, scale, reach, cuts=(), kind=jnp.bfloat16):
    values = scale * jax.random.normal(key, shape, jnp.float32)
    if cuts:
        values = values * steps_of(key, shape, cuts, -0.22, 0.18)
    return jnp.clip(values, -reach, reach).astype(kind)


def setup_inputs(seed: int = 0, part: int = 0) -> dict:
    streams_of = jax.random.split(jax.random.key(seed), 10)
    part_keys = jax.random.split(jax.random.fold_in(streams_of[9], part), 10)
    moe_rows = centred(part_keys[0], (ROWS, D), 1.0, 6.0, ((0, 16),))
    routes_keys = jax.random.split(jax.random.fold_in(part_keys[1], 1), ROWS // ROWS_DEV)
    routes_turns = jax.random.permutation(jax.random.fold_in(part_keys[1], 3), ROWS // ROWS_DEV)
    routes = jax.vmap(lambda own, number: routed_block(jax.random.fold_in(part_keys[1], 2), own, number, ROWS_DEV, EXPERTS, TOP, CAP, 2))(routes_keys, routes_turns).reshape((ROWS, TOP))
    route_weights = jnp.clip(0.05 + 0.45 * jax.random.uniform(part_keys[2], (ROWS, TOP), jnp.float32) ** steps_of(part_keys[2], (ROWS, TOP), ((0, 16),), -0.2, 0.2), 0.05, 0.5)
    w_gate = centred(streams_of[3], (N_EP, D, FF_HALF), D ** -0.5, 0.09375, ((0, 16),))
    w_up = centred(streams_of[4], (N_EP, D, FF_HALF), D ** -0.5, 0.09375, ((0, 16),))
    w_down = centred(streams_of[5], (N_EP, FF_HALF, D), FF ** -0.5, 0.1875, ((0, 16),))
    queries = draw_queries(jax.random.fold_in(jax.random.fold_in(streams_of[9], part), 71), part)
    latent_cache = draw_latent_cache(jax.random.fold_in(jax.random.fold_in(streams_of[9], part), 71), part)
    lengths = draw_lengths(jax.random.fold_in(jax.random.fold_in(streams_of[9], part), 71), part)
    return {"moe_rows": moe_rows, "routes": routes, "route_weights": route_weights, "w_gate": w_gate, "w_up": w_up, "w_down": w_down, "queries": queries, "latent_cache": latent_cache, "lengths": lengths}


score_scale = 192.0 ** -0.5


def attend(queries, latent_cache, lengths):
    scores = jnp.einsum("rhc,rlc->rhl", queries.astype(jnp.float32), latent_cache.astype(jnp.float32)) * score_scale
    in_range = jnp.arange(CTX, dtype=jnp.int32)[None, None, :] < lengths.astype(jnp.int32)[:, None, None]
    scores = jnp.where(in_range, scores, -1e30)
    highest = jnp.max(scores, axis=-1, keepdims=True)
    expo = jnp.where(in_range, jnp.exp(scores - highest), 0.0)
    probs = (expo / jnp.sum(expo, axis=-1, keepdims=True)).astype(jnp.bfloat16)
    values = latent_cache[:, :, :LATENT].astype(jnp.float32)
    return jnp.einsum("rhl,rlc->rhc", probs.astype(jnp.float32), values).astype(jnp.bfloat16)


def reference(moe_rows, routes, route_weights, w_gate, w_up, w_down, queries, latent_cache, lengths):
    attn_out = attend(queries, latent_cache, lengths)
    flat_experts = routes.reshape(-1).astype(jnp.int32)
    slot_total = flat_experts.shape[0]
    ordering = jnp.argsort(flat_experts, stable=True).astype(jnp.int32)
    matches = (flat_experts[:, None] == jnp.arange(EXPERTS, dtype=jnp.int32)[None, :]).astype(jnp.int32)
    counts = jnp.sum(matches, axis=0).astype(jnp.int32)
    starts = (jnp.cumsum(counts) - counts).astype(jnp.int32)
    span_rows = N_EP * CAP
    ordering_pad = jnp.concatenate([ordering, jnp.zeros((span_rows,), jnp.int32)])
    gate_pairs = w_gate.reshape(EXPERTS, 2, D, FF_HALF)
    up_pairs = w_up.reshape(EXPERTS, 2, D, FF_HALF)
    down_pairs = w_down.reshape(EXPERTS, 2 * FF_HALF, D)

    def one_expert(carry, expert):
        picked = lax.dynamic_slice(ordering_pad, (starts[expert],), (span_rows,))
        live_slot = jnp.arange(span_rows, dtype=jnp.int32) < counts[expert]
        inputs = moe_rows[picked // TOP]
        gate_full = jnp.concatenate([gate_pairs[expert, 0], gate_pairs[expert, 1]], axis=1)
        up_full = jnp.concatenate([up_pairs[expert, 0], up_pairs[expert, 1]], axis=1)
        gate_act = jnp.dot(inputs, gate_full, preferred_element_type=jnp.float32)
        up_act = jnp.dot(inputs, up_full, preferred_element_type=jnp.float32)
        hidden = (jax.nn.silu(gate_act) * up_act).astype(jnp.bfloat16)
        result = jnp.dot(hidden, down_pairs[expert], preferred_element_type=jnp.float32).astype(jnp.bfloat16)
        landing = jnp.where(live_slot, picked, slot_total)
        return carry.at[landing].set(result, mode="drop"), None

    slot_out, _ = lax.scan(one_expert, jnp.zeros((slot_total, D), jnp.bfloat16), jnp.arange(EXPERTS, dtype=jnp.int32))
    expert_out = slot_out.reshape(ROWS, TOP, D).astype(jnp.float32)
    moe_out = jnp.einsum("rk,rkd->rd", route_weights.astype(jnp.float32), expert_out).astype(jnp.bfloat16)
    return moe_out, attn_out
```

```python
import jax
import jax.numpy as jnp
from jax import lax
from jax.sharding import PartitionSpec as P

LATENT = 512


score_scale = 192.0 ** (-0.5)


def attend(queries, latent_cache, lengths):
    scores = (
        jnp.einsum("rhc,rlc->rhl", queries, latent_cache, preferred_element_type=jnp.float32)
        * score_scale
    )
    in_range = (
        jnp.arange(latent_cache.shape[1], dtype=jnp.int32)[None, None, :] < lengths[:, None, None]
    )
    scores = jnp.where(in_range, scores, -1e30)
    highest = jnp.max(scores, axis=-1, keepdims=True)
    expo = jnp.where(in_range, jnp.exp(scores - highest), 0.0)
    probs = (expo / jnp.sum(expo, axis=-1, keepdims=True)).astype(jnp.bfloat16)
    return jnp.einsum(
        "rhl,rlc->rhc", probs, latent_cache[:, :, :LATENT], preferred_element_type=jnp.float32
    ).astype(jnp.bfloat16)


def shards(moe_rows, routes, route_weights, w_gate, w_up, w_down, queries, latent_cache, lengths):
    attn_out = attend(queries, latent_cache, lengths)
    expert = lax.axis_index("ep") // 2
    all_rows = lax.all_gather(moe_rows, "ep", axis=0, tiled=True)
    all_routes = lax.all_gather(routes, "ep", axis=0, tiled=True)
    all_weights = lax.all_gather(route_weights, "ep", axis=0, tiled=True)
    weight = jnp.sum(jnp.where(all_routes == expert, all_weights, 0.0), axis=1)
    gate_act = jnp.dot(all_rows, w_gate[0], preferred_element_type=jnp.float32)
    up_act = jnp.dot(all_rows, w_up[0], preferred_element_type=jnp.float32)
    hidden = (jax.nn.silu(gate_act) * up_act).astype(jnp.bfloat16)
    partial_out = jnp.dot(hidden, w_down[0], preferred_element_type=jnp.float32)
    partial_out = partial_out * weight[:, None]
    moe_out = lax.psum_scatter(partial_out, "ep", scatter_dimension=0, tiled=True)
    return (moe_out.astype(jnp.bfloat16), attn_out)


def solution(mesh):
    in_specs = (
        P(("dp", "ep"), None),
        P(("dp", "ep"), None),
        P(("dp", "ep"), None),
        P("ep", None, None),
        P("ep", None, None),
        P("ep", None, None),
        P(("dp", "ep"), None, None),
        P(("dp", "ep"), None, None),
        P(("dp", "ep")),
    )
    out_specs = (P(("dp", "ep"), None), P(("dp", "ep"), None, None))
    return jax.shard_map(shards, mesh=mesh, in_specs=in_specs, out_specs=out_specs, check_vma=False)
```

```python
import jax
import jax.numpy as jnp
from jax import lax
from jax.sharding import PartitionSpec as P

LATENT = 512


score_scale = 192.0 ** (-0.5)


def attend(queries, latent_cache, lengths):
    scores = (
        jnp.einsum("rhc,rlc->rhl", queries, latent_cache, preferred_element_type=jnp.float32)
        * score_scale
    )
    in_range = (
        jnp.arange(latent_cache.shape[1], dtype=jnp.int32)[None, None, :] < lengths[:, None, None]
    )
    scores = jnp.where(in_range, scores, -1e30)
    highest = jnp.max(scores, axis=-1, keepdims=True)
    expo = jnp.where(in_range, jnp.exp(scores - highest), 0.0)
    probs = (expo / jnp.sum(expo, axis=-1, keepdims=True)).astype(jnp.bfloat16)
    return jnp.einsum(
        "rhl,rlc->rhc", probs, latent_cache[:, :, :LATENT], preferred_element_type=jnp.float32
    ).astype(jnp.bfloat16)


def shards(moe_rows, routes, route_weights, w_gate, w_up, w_down, queries, latent_cache, lengths):
    attn_out = attend(queries, latent_cache, lengths)
    rows_here, model_width = moe_rows.shape
    experts = lax.axis_size("ep") // 2
    expert = lax.axis_index("ep") // 2
    named = routes[:, :, None] == jnp.arange(experts, dtype=jnp.int32)[None, None, :]
    dense_w = jnp.sum(jnp.where(named, route_weights[:, :, None], 0.0), axis=1)
    hi = dense_w.astype(jnp.bfloat16)
    rest = dense_w - hi.astype(jnp.float32)
    mid = rest.astype(jnp.bfloat16)
    lo = (rest - mid.astype(jnp.float32)).astype(jnp.bfloat16)
    extra = -(-3 * experts // 128) * 128
    tail = jnp.zeros((rows_here, extra - 3 * experts), jnp.bfloat16)
    packed = jnp.concatenate([moe_rows, hi, mid, lo, tail], axis=1)
    gathered = lax.all_gather(packed, "ep", axis=0, tiled=True)
    all_rows = gathered[:, :model_width]
    parts = gathered[:, model_width:model_width + 3 * experts].astype(jnp.float32)
    parts = parts.reshape(-1, 3, experts)
    weight_all = (parts[:, 0] + (parts[:, 1] + parts[:, 2]))
    weight = jnp.sum(
        jnp.where(jnp.arange(experts)[None, :] == expert, weight_all, 0.0), axis=1
    )
    gate_act = jnp.dot(all_rows, w_gate[0], preferred_element_type=jnp.float32)
    up_act = jnp.dot(all_rows, w_up[0], preferred_element_type=jnp.float32)
    hidden = (jax.nn.silu(gate_act) * up_act).astype(jnp.bfloat16)
    partial_out = jnp.dot(hidden, w_down[0], preferred_element_type=jnp.float32)
    partial_out = partial_out * weight[:, None]
    moe_out = lax.psum_scatter(partial_out, "ep", scatter_dimension=0, tiled=True)
    return (moe_out.astype(jnp.bfloat16), attn_out)


def solution(mesh):
    in_specs = (
        P(("dp", "ep"), None),
        P(("dp", "ep"), None),
        P(("dp", "ep"), None),
        P("ep", None, None),
        P("ep", None, None),
        P("ep", None, None),
        P(("dp", "ep"), None, None),
        P(("dp", "ep"), None, None),
        P(("dp", "ep")),
    )
    out_specs = (P(("dp", "ep"), None), P(("dp", "ep"), None, None))
    return jax.shard_map(shards, mesh=mesh, in_specs=in_specs, out_specs=out_specs, check_vma=False)
```

```python
import jax
import jax.numpy as jnp
from jax import lax
from jax.sharding import PartitionSpec as P

LATENT = 512


score_scale = 192.0 ** (-0.5)


def attend(queries, latent_cache, lengths):
    scores = (
        jnp.einsum("rhc,rlc->rhl", queries, latent_cache, preferred_element_type=jnp.float32)
        * score_scale
    )
    in_range = (
        jnp.arange(latent_cache.shape[1], dtype=jnp.int32)[None, None, :] < lengths[:, None, None]
    )
    scores = jnp.where(in_range, scores, -1e30)
    highest = jnp.max(scores, axis=-1, keepdims=True)
    expo = jnp.where(in_range, jnp.exp(scores - highest), 0.0)
    probs = (expo / jnp.sum(expo, axis=-1, keepdims=True)).astype(jnp.bfloat16)
    return jnp.einsum(
        "rhl,rlc->rhc", probs, latent_cache[:, :, :LATENT], preferred_element_type=jnp.float32
    ).astype(jnp.bfloat16)


def shards(moe_rows, routes, route_weights, w_gate, w_up, w_down, queries, latent_cache, lengths):
    attn_out = attend(queries, latent_cache, lengths)
    rows_here, model_width = moe_rows.shape
    experts = lax.axis_size("ep") // 2
    expert = lax.axis_index("ep") // 2
    named = routes[:, :, None] == jnp.arange(experts, dtype=jnp.int32)[None, None, :]
    dense_w = jnp.sum(jnp.where(named, route_weights[:, :, None], 0.0), axis=1)
    hi = lax.reduce_precision(dense_w, exponent_bits=8, mantissa_bits=7)
    rest = dense_w - hi
    mid = lax.reduce_precision(rest, exponent_bits=8, mantissa_bits=7)
    lo = rest - mid
    hi, mid, lo = (p.astype(jnp.bfloat16) for p in (hi, mid, lo))
    extra = -(-3 * experts // 128) * 128
    tail = jnp.zeros((rows_here, extra - 3 * experts), jnp.bfloat16)
    packed = jnp.concatenate([moe_rows, hi, mid, lo, tail], axis=1)
    gathered = lax.all_gather(packed, "ep", axis=0, tiled=True)
    all_rows = gathered[:, :model_width]
    parts = gathered[:, model_width:model_width + 3 * experts].astype(jnp.float32)
    parts = parts.reshape(-1, 3, experts)
    weight_all = (parts[:, 0] + (parts[:, 1] + parts[:, 2]))
    weight = jnp.sum(
        jnp.where(jnp.arange(experts)[None, :] == expert, weight_all, 0.0), axis=1
    )
    gate_act = jnp.dot(all_rows, w_gate[0], preferred_element_type=jnp.float32)
    up_act = jnp.dot(all_rows, w_up[0], preferred_element_type=jnp.float32)
    hidden = (jax.nn.silu(gate_act) * up_act).astype(jnp.bfloat16)
    partial_out = jnp.dot(hidden, w_down[0], preferred_element_type=jnp.float32)
    partial_out = (partial_out * weight[:, None]).astype(jnp.bfloat16)
    moe_out = lax.psum_scatter(partial_out, "ep", scatter_dimension=0, tiled=True)
    return (moe_out.astype(jnp.bfloat16), attn_out)


def solution(mesh):
    in_specs = (
        P(("dp", "ep"), None),
        P(("dp", "ep"), None),
        P(("dp", "ep"), None),
        P("ep", None, None),
        P("ep", None, None),
        P("ep", None, None),
        P(("dp", "ep"), None, None),
        P(("dp", "ep"), None, None),
        P(("dp", "ep")),
    )
    out_specs = (P(("dp", "ep"), None), P(("dp", "ep"), None, None))
    return jax.shard_map(shards, mesh=mesh, in_specs=in_specs, out_specs=out_specs, check_vma=False)
```

```python
import jax
import jax.numpy as jnp
from jax import lax
from jax.sharding import PartitionSpec as P

LATENT = 512


score_scale = 192.0 ** (-0.5)


def attend(queries, latent_cache, lengths):
    scores = (
        jnp.einsum("rhc,rlc->rhl", queries, latent_cache, preferred_element_type=jnp.float32)
        * score_scale
    )
    in_range = (
        jnp.arange(latent_cache.shape[1], dtype=jnp.int32)[None, None, :] < lengths[:, None, None]
    )
    scores = jnp.where(in_range, scores, -1e30)
    highest = jnp.max(scores, axis=-1, keepdims=True)
    expo = jnp.where(in_range, jnp.exp(scores - highest), 0.0)
    probs = (expo / jnp.sum(expo, axis=-1, keepdims=True)).astype(jnp.bfloat16)
    return jnp.einsum(
        "rhl,rlc->rhc", probs, latent_cache[:, :, :LATENT], preferred_element_type=jnp.float32
    ).astype(jnp.bfloat16)


def halving_reduce_scatter(x, axis):
    n = lax.axis_size(axis)
    me = lax.axis_index(axis)
    cur = x.reshape(n, x.shape[0] // n, x.shape[1])
    bit = 1
    while bit < n:
        pairs = cur.reshape(cur.shape[0] // 2, 2, *cur.shape[1:])
        mine = (me // bit) % 2
        keep = lax.dynamic_index_in_dim(pairs, mine, axis=1, keepdims=False)
        send = lax.dynamic_index_in_dim(pairs, 1 - mine, axis=1, keepdims=False)
        got = lax.ppermute(
            send.astype(jnp.bfloat16), axis, [(j, j ^ bit) for j in range(n)]
        )
        cur = keep.astype(jnp.float32) + got.astype(jnp.float32)
        bit *= 2
    return cur[0]


def shards(moe_rows, routes, route_weights, w_gate, w_up, w_down, queries, latent_cache, lengths):
    attn_out = attend(queries, latent_cache, lengths)
    rows_here, model_width = moe_rows.shape
    experts = lax.axis_size("ep") // 2
    expert = lax.axis_index("ep") // 2
    named = routes[:, :, None] == jnp.arange(experts, dtype=jnp.int32)[None, None, :]
    dense_w = jnp.sum(jnp.where(named, route_weights[:, :, None], 0.0), axis=1)
    hi = lax.reduce_precision(dense_w, exponent_bits=8, mantissa_bits=7)
    rest = dense_w - hi
    mid = lax.reduce_precision(rest, exponent_bits=8, mantissa_bits=7)
    lo = rest - mid
    hi, mid, lo = (p.astype(jnp.bfloat16) for p in (hi, mid, lo))
    extra = -(-3 * experts // 128) * 128
    tail = jnp.zeros((rows_here, extra - 3 * experts), jnp.bfloat16)
    packed = jnp.concatenate([moe_rows, hi, mid, lo, tail], axis=1)
    gathered = lax.all_gather(packed, "ep", axis=0, tiled=True)
    all_rows = gathered[:, :model_width]
    parts = gathered[:, model_width:model_width + 3 * experts].astype(jnp.float32)
    parts = parts.reshape(-1, 3, experts)
    weight_all = (parts[:, 0] + (parts[:, 1] + parts[:, 2]))
    weight = jnp.sum(
        jnp.where(jnp.arange(experts)[None, :] == expert, weight_all, 0.0), axis=1
    )
    gate_act = jnp.dot(all_rows, w_gate[0], preferred_element_type=jnp.float32)
    up_act = jnp.dot(all_rows, w_up[0], preferred_element_type=jnp.float32)
    hidden = (jax.nn.silu(gate_act) * up_act).astype(jnp.bfloat16)
    partial_out = jnp.dot(hidden, w_down[0], preferred_element_type=jnp.float32)
    partial_out = partial_out * weight[:, None]
    moe_out = halving_reduce_scatter(partial_out, "ep")
    return (moe_out.astype(jnp.bfloat16), attn_out)


def solution(mesh):
    in_specs = (
        P(("dp", "ep"), None),
        P(("dp", "ep"), None),
        P(("dp", "ep"), None),
        P("ep", None, None),
        P("ep", None, None),
        P("ep", None, None),
        P(("dp", "ep"), None, None),
        P(("dp", "ep"), None, None),
        P(("dp", "ep")),
    )
    out_specs = (P(("dp", "ep"), None), P(("dp", "ep"), None, None))
    return jax.shard_map(shards, mesh=mesh, in_specs=in_specs, out_specs=out_specs, check_vma=False)
```

```python
import jax
import jax.numpy as jnp
from jax import lax
from jax.sharding import PartitionSpec as P

LATENT = 512


score_scale = 192.0 ** (-0.5)


def attend(queries, latent_cache, lengths):
    scores = (
        jnp.einsum("rhc,rlc->rhl", queries, latent_cache, preferred_element_type=jnp.float32)
        * score_scale
    )
    in_range = (
        jnp.arange(latent_cache.shape[1], dtype=jnp.int32)[None, None, :] < lengths[:, None, None]
    )
    scores = jnp.where(in_range, scores, -1e30)
    highest = jnp.max(scores, axis=-1, keepdims=True)
    expo = jnp.where(in_range, jnp.exp(scores - highest), 0.0)
    probs = (expo / jnp.sum(expo, axis=-1, keepdims=True)).astype(jnp.bfloat16)
    return jnp.einsum(
        "rhl,rlc->rhc", probs, latent_cache[:, :, :LATENT], preferred_element_type=jnp.float32
    ).astype(jnp.bfloat16)


def _swap01(t, bits):
    return {0: 1, 1: 0}.get(t, t) if bits > 1 else t


def halving_reduce_scatter(x, axis):
    n = lax.axis_size(axis)
    chips = n // 2
    bits = chips.bit_length() - 1
    me = lax.axis_index(axis)
    core, chip = me % 2, me // 2
    blocks = x.reshape(n, x.shape[0] // n, x.shape[1])
    plain = jnp.arange(chips, dtype=jnp.int32)
    swapped = sum(((plain >> t) & 1) << _swap01(t, bits) for t in range(bits))
    mine = jnp.where(core == 0, plain, swapped)
    theirs = jnp.where(core == 0, swapped, plain)
    keep = jnp.take(blocks, 2 * mine + core, axis=0)
    send = jnp.take(blocks, 2 * theirs + (1 - core), axis=0)
    got = lax.ppermute(send.astype(jnp.bfloat16), axis, [(j, j ^ 1) for j in range(n)])
    cur = keep.astype(jnp.float32) + got.astype(jnp.float32)
    for t in range(bits):
        order = jnp.where(core == 0, t, _swap01(t, bits))
        bit_here = (chip >> order) & 1
        pairs = cur.reshape(cur.shape[0] // 2, 2, *cur.shape[1:])
        keep = lax.dynamic_index_in_dim(pairs, bit_here, axis=1, keepdims=False)
        send = lax.dynamic_index_in_dim(pairs, 1 - bit_here, axis=1, keepdims=False)
        partner = [(j, j ^ (2 << (t if j % 2 == 0 else _swap01(t, bits)))) for j in range(n)]
        got = lax.ppermute(send.astype(jnp.bfloat16), axis, partner)
        cur = keep.astype(jnp.float32) + got.astype(jnp.float32)
    return cur[0]


def shards(moe_rows, routes, route_weights, w_gate, w_up, w_down, queries, latent_cache, lengths):
    attn_out = attend(queries, latent_cache, lengths)
    rows_here, model_width = moe_rows.shape
    experts = lax.axis_size("ep") // 2
    expert = lax.axis_index("ep") // 2
    named = routes[:, :, None] == jnp.arange(experts, dtype=jnp.int32)[None, None, :]
    dense_w = jnp.sum(jnp.where(named, route_weights[:, :, None], 0.0), axis=1)
    hi = lax.reduce_precision(dense_w, exponent_bits=8, mantissa_bits=7)
    rest = dense_w - hi
    mid = lax.reduce_precision(rest, exponent_bits=8, mantissa_bits=7)
    lo = rest - mid
    hi, mid, lo = (p.astype(jnp.bfloat16) for p in (hi, mid, lo))
    extra = -(-3 * experts // 128) * 128
    tail = jnp.zeros((rows_here, extra - 3 * experts), jnp.bfloat16)
    packed = jnp.concatenate([moe_rows, hi, mid, lo, tail], axis=1)
    gathered = lax.all_gather(packed, "ep", axis=0, tiled=True)
    all_rows = gathered[:, :model_width]
    parts = gathered[:, model_width:model_width + 3 * experts].astype(jnp.float32)
    parts = parts.reshape(-1, 3, experts)
    weight_all = (parts[:, 0] + (parts[:, 1] + parts[:, 2]))
    weight = jnp.sum(
        jnp.where(jnp.arange(experts)[None, :] == expert, weight_all, 0.0), axis=1
    )
    gate_act = jnp.dot(all_rows, w_gate[0], preferred_element_type=jnp.float32)
    up_act = jnp.dot(all_rows, w_up[0], preferred_element_type=jnp.float32)
    hidden = (jax.nn.silu(gate_act) * up_act).astype(jnp.bfloat16)
    partial_out = jnp.dot(hidden, w_down[0], preferred_element_type=jnp.float32)
    partial_out = partial_out * weight[:, None]
    moe_out = halving_reduce_scatter(partial_out, "ep")
    return (moe_out.astype(jnp.bfloat16), attn_out)


def solution(mesh):
    in_specs = (
        P(("dp", "ep"), None),
        P(("dp", "ep"), None),
        P(("dp", "ep"), None),
        P("ep", None, None),
        P("ep", None, None),
        P("ep", None, None),
        P(("dp", "ep"), None, None),
        P(("dp", "ep"), None, None),
        P(("dp", "ep")),
    )
    out_specs = (P(("dp", "ep"), None), P(("dp", "ep"), None, None))
    return jax.shard_map(shards, mesh=mesh, in_specs=in_specs, out_specs=out_specs, check_vma=False)
```

```python
import jax
import jax.numpy as jnp
from jax import lax
from jax.sharding import PartitionSpec as P

LATENT = 512


score_scale = 192.0 ** (-0.5)


def attend(queries, latent_cache, lengths):
    scores = (
        jnp.einsum("rhc,rlc->rhl", queries, latent_cache, preferred_element_type=jnp.float32)
        * score_scale
    )
    in_range = (
        jnp.arange(latent_cache.shape[1], dtype=jnp.int32)[None, None, :] < lengths[:, None, None]
    )
    scores = jnp.where(in_range, scores, -1e30)
    highest = jnp.max(scores, axis=-1, keepdims=True)
    expo = jnp.where(in_range, jnp.exp(scores - highest), 0.0)
    probs = (expo / jnp.sum(expo, axis=-1, keepdims=True)).astype(jnp.bfloat16)
    return jnp.einsum(
        "rhl,rlc->rhc", probs, latent_cache[:, :, :LATENT], preferred_element_type=jnp.float32
    ).astype(jnp.bfloat16)


def _swap01(t, bits):
    return {0: 1, 1: 0}.get(t, t) if bits > 1 else t


def first_split(axis, rows_per_block):
    n = lax.axis_size(axis)
    chips = n // 2
    bits = chips.bit_length() - 1
    core = lax.axis_index(axis) % 2
    plain = jnp.arange(chips, dtype=jnp.int32)
    swapped = sum(((plain >> t) & 1) << _swap01(t, bits) for t in range(bits))
    mine = jnp.where(core == 0, plain, swapped)
    theirs = jnp.where(core == 0, swapped, plain)
    within = jnp.arange(rows_per_block, dtype=jnp.int32)[None, :]
    keep = ((2 * mine + core)[:, None] * rows_per_block + within).reshape(-1)
    send = ((2 * theirs + (1 - core))[:, None] * rows_per_block + within).reshape(-1)
    return keep, send


def halving_rest(keep, send, axis):
    n = lax.axis_size(axis)
    chips = n // 2
    bits = chips.bit_length() - 1
    me = lax.axis_index(axis)
    core, chip = me % 2, me // 2
    got = lax.ppermute(send, axis, [(j, j ^ 1) for j in range(n)])
    cur = (keep + got.astype(jnp.float32)).reshape(chips, -1, keep.shape[-1])
    for t in range(bits):
        order = jnp.where(core == 0, t, _swap01(t, bits))
        bit_here = (chip >> order) & 1
        pairs = cur.reshape(cur.shape[0] // 2, 2, *cur.shape[1:])
        kept = lax.dynamic_index_in_dim(pairs, bit_here, axis=1, keepdims=False)
        sent = lax.dynamic_index_in_dim(pairs, 1 - bit_here, axis=1, keepdims=False)
        partner = [(j, j ^ (2 << (t if j % 2 == 0 else _swap01(t, bits)))) for j in range(n)]
        got = lax.ppermute(sent.astype(jnp.bfloat16), axis, partner)
        cur = kept + got.astype(jnp.float32)
    return cur[0]


def shards(moe_rows, routes, route_weights, w_gate, w_up, w_down, queries, latent_cache, lengths):
    attn_out = attend(queries, latent_cache, lengths)
    rows_here, model_width = moe_rows.shape
    experts = lax.axis_size("ep") // 2
    expert = lax.axis_index("ep") // 2
    named = routes[:, :, None] == jnp.arange(experts, dtype=jnp.int32)[None, None, :]
    dense_w = jnp.sum(jnp.where(named, route_weights[:, :, None], 0.0), axis=1)
    hi = lax.reduce_precision(dense_w, exponent_bits=8, mantissa_bits=7)
    rest = dense_w - hi
    mid = lax.reduce_precision(rest, exponent_bits=8, mantissa_bits=7)
    lo = rest - mid
    hi, mid, lo = (p.astype(jnp.bfloat16) for p in (hi, mid, lo))
    extra = -(-3 * experts // 128) * 128
    tail = jnp.zeros((rows_here, extra - 3 * experts), jnp.bfloat16)
    packed = jnp.concatenate([moe_rows, hi, mid, lo, tail], axis=1)
    gathered = lax.all_gather(packed, "ep", axis=0, tiled=True)
    all_rows = gathered[:, :model_width]
    parts = gathered[:, model_width:model_width + 3 * experts].astype(jnp.float32)
    parts = parts.reshape(-1, 3, experts)
    weight_all = (parts[:, 0] + (parts[:, 1] + parts[:, 2]))
    weight = jnp.sum(
        jnp.where(jnp.arange(experts)[None, :] == expert, weight_all, 0.0), axis=1
    )
    gate_act = jnp.dot(all_rows, w_gate[0], preferred_element_type=jnp.float32)
    up_act = jnp.dot(all_rows, w_up[0], preferred_element_type=jnp.float32)
    hidden = (jax.nn.silu(gate_act) * up_act).astype(jnp.bfloat16)
    keep_rows, send_rows = first_split("ep", rows_here)
    send = jnp.dot(jnp.take(hidden, send_rows, axis=0), w_down[0], preferred_element_type=jnp.float32)
    send = (send * jnp.take(weight, send_rows)[:, None]).astype(jnp.bfloat16)
    keep = jnp.dot(jnp.take(hidden, keep_rows, axis=0), w_down[0], preferred_element_type=jnp.float32)
    keep = keep * jnp.take(weight, keep_rows)[:, None]
    moe_out = halving_rest(keep, send, "ep")
    return (moe_out.astype(jnp.bfloat16), attn_out)


def solution(mesh):
    in_specs = (
        P(("dp", "ep"), None),
        P(("dp", "ep"), None),
        P(("dp", "ep"), None),
        P("ep", None, None),
        P("ep", None, None),
        P("ep", None, None),
        P(("dp", "ep"), None, None),
        P(("dp", "ep"), None, None),
        P(("dp", "ep")),
    )
    out_specs = (P(("dp", "ep"), None), P(("dp", "ep"), None, None))
    return jax.shard_map(shards, mesh=mesh, in_specs=in_specs, out_specs=out_specs, check_vma=False)
```

```python
import jax
import numpy as np
import jax.numpy as jnp
from jax import lax
from jax.sharding import PartitionSpec as P

LATENT = 512


score_scale = 192.0 ** (-0.5)


def attend(queries, latent_cache, lengths):
    scores = (
        jnp.einsum("rhc,rlc->rhl", queries, latent_cache, preferred_element_type=jnp.float32)
        * score_scale
    )
    in_range = (
        jnp.arange(latent_cache.shape[1], dtype=jnp.int32)[None, None, :] < lengths[:, None, None]
    )
    scores = jnp.where(in_range, scores, -1e30)
    highest = jnp.max(scores, axis=-1, keepdims=True)
    expo = jnp.where(in_range, jnp.exp(scores - highest), 0.0)
    probs = (expo / jnp.sum(expo, axis=-1, keepdims=True)).astype(jnp.bfloat16)
    return jnp.einsum(
        "rhl,rlc->rhc", probs, latent_cache[:, :, :LATENT], preferred_element_type=jnp.float32
    ).astype(jnp.bfloat16)


def _swap01(t, bits):
    return {0: 1, 1: 0}.get(t, t) if bits > 1 else t


def _orders(bits):
    return [list(range(bits)), [_swap01(t, bits) for t in range(bits)]]


def gather_positions(n):
    chips = n // 2
    bits = chips.bit_length() - 1
    orders = [list(reversed(o)) for o in _orders(bits)]
    table = np.zeros((n,), np.int32)
    for j in range(n):
        group, chip = j % 2, j // 2
        place = sum(((chip >> orders[group][t]) & 1) << t for t in range(bits))
        table[j] = group * chips + place
    return table


def doubling_gather(block, axis):
    n = lax.axis_size(axis)
    chips = n // 2
    bits = chips.bit_length() - 1
    me = lax.axis_index(axis)
    core, chip = me % 2, me // 2
    orders = [list(reversed(o)) for o in _orders(bits)]
    cur = block[None]
    for t in range(bits):
        bit_here = (chip >> jnp.where(core == 0, orders[0][t], orders[1][t])) & 1
        partner = [(j, j ^ (2 << orders[j % 2][t])) for j in range(n)]
        got = lax.ppermute(cur, axis, partner)
        cur = jnp.where(bit_here == 0, jnp.concatenate([cur, got]), jnp.concatenate([got, cur]))
    other = lax.ppermute(cur, axis, [(j, j ^ 1) for j in range(n)])
    full = jnp.where(core == 0, jnp.concatenate([cur, other]), jnp.concatenate([other, cur]))
    return full.reshape(n * block.shape[0], block.shape[1])


def first_split(axis, rows_per_block):
    n = lax.axis_size(axis)
    chips = n // 2
    bits = chips.bit_length() - 1
    core = lax.axis_index(axis) % 2
    plain = jnp.arange(chips, dtype=jnp.int32)
    swapped = sum(((plain >> t) & 1) << _swap01(t, bits) for t in range(bits))
    mine = jnp.where(core == 0, plain, swapped)
    theirs = jnp.where(core == 0, swapped, plain)
    within = jnp.arange(rows_per_block, dtype=jnp.int32)[None, :]
    place = jnp.asarray(gather_positions(n))
    keep = (place[2 * mine + core][:, None] * rows_per_block + within).reshape(-1)
    send = (place[2 * theirs + (1 - core)][:, None] * rows_per_block + within).reshape(-1)
    return keep, send


def halving_rest(keep, send, axis):
    n = lax.axis_size(axis)
    chips = n // 2
    bits = chips.bit_length() - 1
    me = lax.axis_index(axis)
    core, chip = me % 2, me // 2
    got = lax.ppermute(send, axis, [(j, j ^ 1) for j in range(n)])
    cur = (keep + got.astype(jnp.float32)).reshape(chips, -1, keep.shape[-1])
    for t in range(bits):
        order = jnp.where(core == 0, t, _swap01(t, bits))
        bit_here = (chip >> order) & 1
        pairs = cur.reshape(cur.shape[0] // 2, 2, *cur.shape[1:])
        kept = lax.dynamic_index_in_dim(pairs, bit_here, axis=1, keepdims=False)
        sent = lax.dynamic_index_in_dim(pairs, 1 - bit_here, axis=1, keepdims=False)
        partner = [(j, j ^ (2 << (t if j % 2 == 0 else _swap01(t, bits)))) for j in range(n)]
        got = lax.ppermute(sent.astype(jnp.bfloat16), axis, partner)
        cur = kept + got.astype(jnp.float32)
    return cur[0]


def shards(moe_rows, routes, route_weights, w_gate, w_up, w_down, queries, latent_cache, lengths):
    attn_out = attend(queries, latent_cache, lengths)
    rows_here, model_width = moe_rows.shape
    experts = lax.axis_size("ep") // 2
    expert = lax.axis_index("ep") // 2
    named = routes[:, :, None] == jnp.arange(experts, dtype=jnp.int32)[None, None, :]
    dense_w = jnp.sum(jnp.where(named, route_weights[:, :, None], 0.0), axis=1)
    hi = lax.reduce_precision(dense_w, exponent_bits=8, mantissa_bits=7)
    rest = dense_w - hi
    mid = lax.reduce_precision(rest, exponent_bits=8, mantissa_bits=7)
    lo = rest - mid
    hi, mid, lo = (p.astype(jnp.bfloat16) for p in (hi, mid, lo))
    extra = -(-3 * experts // 128) * 128
    tail = jnp.zeros((rows_here, extra - 3 * experts), jnp.bfloat16)
    packed = jnp.concatenate([moe_rows, hi, mid, lo, tail], axis=1)
    gathered = doubling_gather(packed, "ep")
    all_rows = gathered[:, :model_width]
    parts = gathered[:, model_width:model_width + 3 * experts].astype(jnp.float32)
    parts = parts.reshape(-1, 3, experts)
    weight_all = (parts[:, 0] + (parts[:, 1] + parts[:, 2]))
    weight = jnp.sum(
        jnp.where(jnp.arange(experts)[None, :] == expert, weight_all, 0.0), axis=1
    )
    gate_act = jnp.dot(all_rows, w_gate[0], preferred_element_type=jnp.float32)
    up_act = jnp.dot(all_rows, w_up[0], preferred_element_type=jnp.float32)
    hidden = (jax.nn.silu(gate_act) * up_act).astype(jnp.bfloat16)
    keep_rows, send_rows = first_split("ep", rows_here)
    send = jnp.dot(jnp.take(hidden, send_rows, axis=0), w_down[0], preferred_element_type=jnp.float32)
    send = (send * jnp.take(weight, send_rows)[:, None]).astype(jnp.bfloat16)
    keep = jnp.dot(jnp.take(hidden, keep_rows, axis=0), w_down[0], preferred_element_type=jnp.float32)
    keep = keep * jnp.take(weight, keep_rows)[:, None]
    moe_out = halving_rest(keep, send, "ep")
    return (moe_out.astype(jnp.bfloat16), attn_out)


def solution(mesh):
    in_specs = (
        P(("dp", "ep"), None),
        P(("dp", "ep"), None),
        P(("dp", "ep"), None),
        P("ep", None, None),
        P("ep", None, None),
        P("ep", None, None),
        P(("dp", "ep"), None, None),
        P(("dp", "ep"), None, None),
        P(("dp", "ep")),
    )
    out_specs = (P(("dp", "ep"), None), P(("dp", "ep"), None, None))
    return jax.shard_map(shards, mesh=mesh, in_specs=in_specs, out_specs=out_specs, check_vma=False)
```

```python
import jax
import jax.numpy as jnp
from jax import lax
from jax.sharding import PartitionSpec as P

LATENT = 512


score_scale = 192.0 ** (-0.5)


def attend(queries, latent_cache, lengths):
    scores = (
        jnp.einsum("rhc,rlc->rhl", queries, latent_cache, preferred_element_type=jnp.float32)
        * score_scale
    )
    in_range = (
        jnp.arange(latent_cache.shape[1], dtype=jnp.int32)[None, None, :] < lengths[:, None, None]
    )
    scores = jnp.where(in_range, scores, -1e30)
    highest = jnp.max(scores, axis=-1, keepdims=True)
    expo = jnp.where(in_range, jnp.exp(scores - highest), 0.0)
    probs = (expo / jnp.sum(expo, axis=-1, keepdims=True)).astype(jnp.bfloat16)
    return jnp.einsum(
        "rhl,rlc->rhc", probs, latent_cache[:, :, :LATENT], preferred_element_type=jnp.float32
    ).astype(jnp.bfloat16)


def _swap01(t, bits):
    return {0: 1, 1: 0}.get(t, t) if bits > 1 else t


def _orders(bits):
    return [list(range(bits)), [_swap01(t, bits) for t in range(bits)]]


def doubling_gather(block, axis):
    n = lax.axis_size(axis)
    chips = n // 2
    bits = chips.bit_length() - 1
    me = lax.axis_index(axis)
    core, chip = me % 2, me // 2
    orders = _orders(bits)
    cur = block[None]
    for k in reversed(range(bits)):
        bit_here = (chip >> jnp.where(core == 0, orders[0][k], orders[1][k])) & 1
        partner = [(j, j ^ (2 << orders[j % 2][k])) for j in range(n)]
        got = lax.ppermute(cur, axis, partner)
        pair = jnp.where(bit_here == 0, jnp.stack([cur, got], axis=1), jnp.stack([got, cur], axis=1))
        cur = pair.reshape(2 * cur.shape[0], *cur.shape[1:])
    other = lax.ppermute(cur, axis, [(j, j ^ 1) for j in range(n)])
    width = block.shape[1]
    return cur.reshape(-1, width), other.reshape(-1, width)


def halving_rest(keep, send, axis):
    n = lax.axis_size(axis)
    chips = n // 2
    bits = chips.bit_length() - 1
    me = lax.axis_index(axis)
    core, chip = me % 2, me // 2
    got = lax.ppermute(send, axis, [(j, j ^ 1) for j in range(n)])
    cur = (keep + got.astype(jnp.float32)).reshape(chips, -1, keep.shape[-1])
    for t in range(bits):
        order = jnp.where(core == 0, t, _swap01(t, bits))
        bit_here = (chip >> order) & 1
        pairs = cur.reshape(cur.shape[0] // 2, 2, *cur.shape[1:])
        kept = lax.dynamic_index_in_dim(pairs, bit_here, axis=1, keepdims=False)
        sent = lax.dynamic_index_in_dim(pairs, 1 - bit_here, axis=1, keepdims=False)
        partner = [(j, j ^ (2 << (t if j % 2 == 0 else _swap01(t, bits)))) for j in range(n)]
        got = lax.ppermute(sent.astype(jnp.bfloat16), axis, partner)
        cur = kept + got.astype(jnp.float32)
    return cur[0]


def expert_hidden(packed, w_gate, w_up, model_width, experts, expert):
    rows = packed[:, :model_width]
    parts = packed[:, model_width:model_width + 3 * experts].astype(jnp.float32)
    parts = parts.reshape(-1, 3, experts)
    weight_all = parts[:, 0] + (parts[:, 1] + parts[:, 2])
    weight = jnp.sum(jnp.where(jnp.arange(experts)[None, :] == expert, weight_all, 0.0), axis=1)
    gate_act = jnp.dot(rows, w_gate, preferred_element_type=jnp.float32)
    up_act = jnp.dot(rows, w_up, preferred_element_type=jnp.float32)
    hidden = (jax.nn.silu(gate_act) * up_act).astype(jnp.bfloat16)
    return hidden, weight


def shards(moe_rows, routes, route_weights, w_gate, w_up, w_down, queries, latent_cache, lengths):
    attn_out = attend(queries, latent_cache, lengths)
    rows_here, model_width = moe_rows.shape
    experts = lax.axis_size("ep") // 2
    expert = lax.axis_index("ep") // 2
    named = routes[:, :, None] == jnp.arange(experts, dtype=jnp.int32)[None, None, :]
    dense_w = jnp.sum(jnp.where(named, route_weights[:, :, None], 0.0), axis=1)
    hi = lax.reduce_precision(dense_w, exponent_bits=8, mantissa_bits=7)
    rest = dense_w - hi
    mid = lax.reduce_precision(rest, exponent_bits=8, mantissa_bits=7)
    lo = rest - mid
    hi, mid, lo = (p.astype(jnp.bfloat16) for p in (hi, mid, lo))
    extra = -(-3 * experts // 128) * 128
    tail = jnp.zeros((rows_here, extra - 3 * experts), jnp.bfloat16)
    packed = jnp.concatenate([moe_rows, hi, mid, lo, tail], axis=1)
    own, other = doubling_gather(packed, "ep")
    args = (w_gate[0], w_up[0], model_width, experts, expert)
    keep_hidden, keep_weight = expert_hidden(own, *args)
    send_hidden, send_weight = expert_hidden(other, *args)
    send = jnp.dot(send_hidden, w_down[0], preferred_element_type=jnp.float32)
    send = (send * send_weight[:, None]).astype(jnp.bfloat16)
    keep = jnp.dot(keep_hidden, w_down[0], preferred_element_type=jnp.float32)
    keep = keep * keep_weight[:, None]
    moe_out = halving_rest(keep, send, "ep")
    return (moe_out.astype(jnp.bfloat16), attn_out)


def solution(mesh):
    in_specs = (
        P(("dp", "ep"), None),
        P(("dp", "ep"), None),
        P(("dp", "ep"), None),
        P("ep", None, None),
        P("ep", None, None),
        P("ep", None, None),
        P(("dp", "ep"), None, None),
        P(("dp", "ep"), None, None),
        P(("dp", "ep")),
    )
    out_specs = (P(("dp", "ep"), None), P(("dp", "ep"), None, None))
    return jax.shard_map(shards, mesh=mesh, in_specs=in_specs, out_specs=out_specs, check_vma=False)
```

```python
import jax
import jax.numpy as jnp
from jax import lax
from jax.sharding import PartitionSpec as P

LATENT = 512


score_scale = 192.0 ** (-0.5)


def attend(queries, latent_cache, lengths):
    scores = (
        jnp.einsum("rhc,rlc->rhl", queries, latent_cache, preferred_element_type=jnp.float32)
        * score_scale
    )
    in_range = (
        jnp.arange(latent_cache.shape[1], dtype=jnp.int32)[None, None, :] < lengths[:, None, None]
    )
    scores = jnp.where(in_range, scores, -1e30)
    highest = jnp.max(scores, axis=-1, keepdims=True)
    expo = jnp.where(in_range, jnp.exp(scores - highest), 0.0)
    probs = (expo / jnp.sum(expo, axis=-1, keepdims=True)).astype(jnp.bfloat16)
    return jnp.einsum(
        "rhl,rlc->rhc", probs, latent_cache[:, :, :LATENT], preferred_element_type=jnp.float32
    ).astype(jnp.bfloat16)


def _swap01(t, bits):
    return {0: 1, 1: 0}.get(t, t) if bits > 1 else t


def _orders(bits):
    return [list(range(bits)), [_swap01(t, bits) for t in range(bits)]]


def _interleave(a, b, bit):
    pair = jnp.where(bit == 0, jnp.stack([a, b], axis=1), jnp.stack([b, a], axis=1))
    return pair.reshape(2 * a.shape[0], *a.shape[1:])


def doubling_gather(block, axis, work):
    n = lax.axis_size(axis)
    chips = n // 2
    bits = chips.bit_length() - 1
    me = lax.axis_index(axis)
    core, chip = me % 2, me // 2
    orders = _orders(bits)
    cur = block[None]
    done = [r[None] for r in work(block)]
    for k in reversed(range(bits)):
        bit_here = (chip >> jnp.where(core == 0, orders[0][k], orders[1][k])) & 1
        partner = [(j, j ^ (2 << orders[j % 2][k])) for j in range(n)]
        got = lax.ppermute(cur, axis, partner)
        fresh = work(got.reshape(-1, block.shape[1]))
        fresh = [r.reshape(got.shape[0], block.shape[0], *r.shape[1:]) for r in fresh]
        done = [_interleave(d, f, bit_here) for d, f in zip(done, fresh)]
        cur = _interleave(cur, got, bit_here)
    other = lax.ppermute(cur, axis, [(j, j ^ 1) for j in range(n)])
    done = [d.reshape(-1, *d.shape[2:]) for d in done]
    return done, other.reshape(-1, block.shape[1])


def halving_rest(keep, send, axis):
    n = lax.axis_size(axis)
    chips = n // 2
    bits = chips.bit_length() - 1
    me = lax.axis_index(axis)
    core, chip = me % 2, me // 2
    got = lax.ppermute(send, axis, [(j, j ^ 1) for j in range(n)])
    cur = (keep + got.astype(jnp.float32)).reshape(chips, -1, keep.shape[-1])
    for t in range(bits):
        order = jnp.where(core == 0, t, _swap01(t, bits))
        bit_here = (chip >> order) & 1
        pairs = cur.reshape(cur.shape[0] // 2, 2, *cur.shape[1:])
        kept = lax.dynamic_index_in_dim(pairs, bit_here, axis=1, keepdims=False)
        sent = lax.dynamic_index_in_dim(pairs, 1 - bit_here, axis=1, keepdims=False)
        partner = [(j, j ^ (2 << (t if j % 2 == 0 else _swap01(t, bits)))) for j in range(n)]
        got = lax.ppermute(sent.astype(jnp.bfloat16), axis, partner)
        cur = kept + got.astype(jnp.float32)
    return cur[0]


def expert_hidden(packed, w_gate, w_up, model_width, experts, expert):
    rows = packed[:, :model_width]
    parts = packed[:, model_width:model_width + 3 * experts].astype(jnp.float32)
    parts = parts.reshape(-1, 3, experts)
    weight_all = parts[:, 0] + (parts[:, 1] + parts[:, 2])
    weight = jnp.sum(jnp.where(jnp.arange(experts)[None, :] == expert, weight_all, 0.0), axis=1)
    gate_act = jnp.dot(rows, w_gate, preferred_element_type=jnp.float32)
    up_act = jnp.dot(rows, w_up, preferred_element_type=jnp.float32)
    hidden = (jax.nn.silu(gate_act) * up_act).astype(jnp.bfloat16)
    return hidden, weight


def shards(moe_rows, routes, route_weights, w_gate, w_up, w_down, queries, latent_cache, lengths):
    attn_out = attend(queries, latent_cache, lengths)
    rows_here, model_width = moe_rows.shape
    experts = lax.axis_size("ep") // 2
    expert = lax.axis_index("ep") // 2
    named = routes[:, :, None] == jnp.arange(experts, dtype=jnp.int32)[None, None, :]
    dense_w = jnp.sum(jnp.where(named, route_weights[:, :, None], 0.0), axis=1)
    hi = lax.reduce_precision(dense_w, exponent_bits=8, mantissa_bits=7)
    rest = dense_w - hi
    mid = lax.reduce_precision(rest, exponent_bits=8, mantissa_bits=7)
    lo = rest - mid
    hi, mid, lo = (p.astype(jnp.bfloat16) for p in (hi, mid, lo))
    extra = -(-3 * experts // 128) * 128
    tail = jnp.zeros((rows_here, extra - 3 * experts), jnp.bfloat16)
    packed = jnp.concatenate([moe_rows, hi, mid, lo, tail], axis=1)
    args = (w_gate[0], w_up[0], model_width, experts, expert)
    (keep_hidden, keep_weight), other = doubling_gather(
        packed, "ep", lambda rows: expert_hidden(rows, *args)
    )
    keep = jnp.dot(keep_hidden, w_down[0], preferred_element_type=jnp.float32)
    keep = keep * keep_weight[:, None]
    keep, other = lax.optimization_barrier((keep, other))
    send_hidden, send_weight = expert_hidden(other, *args)
    send = jnp.dot(send_hidden, w_down[0], preferred_element_type=jnp.float32)
    send = (send * send_weight[:, None]).astype(jnp.bfloat16)
    moe_out = halving_rest(keep, send, "ep")
    return (moe_out.astype(jnp.bfloat16), attn_out)


def solution(mesh):
    in_specs = (
        P(("dp", "ep"), None),
        P(("dp", "ep"), None),
        P(("dp", "ep"), None),
        P("ep", None, None),
        P("ep", None, None),
        P("ep", None, None),
        P(("dp", "ep"), None, None),
        P(("dp", "ep"), None, None),
        P(("dp", "ep")),
    )
    out_specs = (P(("dp", "ep"), None), P(("dp", "ep"), None, None))
    return jax.shard_map(shards, mesh=mesh, in_specs=in_specs, out_specs=out_specs, check_vma=False)
```

```python
import jax
import jax.numpy as jnp
from jax import lax
from jax.sharding import PartitionSpec as P

LATENT = 512


score_scale = 192.0 ** (-0.5)


def attend(queries, latent_cache, lengths):
    scores = (
        jnp.einsum("rhc,rlc->rhl", queries, latent_cache, preferred_element_type=jnp.float32)
        * score_scale
    )
    in_range = (
        jnp.arange(latent_cache.shape[1], dtype=jnp.int32)[None, None, :] < lengths[:, None, None]
    )
    scores = jnp.where(in_range, scores, -1e30)
    highest = jnp.max(scores, axis=-1, keepdims=True)
    expo = jnp.where(in_range, jnp.exp(scores - highest), 0.0)
    probs = (expo / jnp.sum(expo, axis=-1, keepdims=True)).astype(jnp.bfloat16)
    return jnp.einsum(
        "rhl,rlc->rhc", probs, latent_cache[:, :, :LATENT], preferred_element_type=jnp.float32
    ).astype(jnp.bfloat16)


def _swap01(t, bits):
    return {0: 1, 1: 0}.get(t, t) if bits > 1 else t


def _orders(bits):
    return [list(range(bits)), [_swap01(t, bits) for t in range(bits)]]


def _interleave(a, b, bit):
    pair = jnp.where(bit == 0, jnp.stack([a, b], axis=1), jnp.stack([b, a], axis=1))
    return pair.reshape(2 * a.shape[0], *a.shape[1:])


def doubling_gather(block, axis, work):
    n = lax.axis_size(axis)
    chips = n // 2
    bits = chips.bit_length() - 1
    me = lax.axis_index(axis)
    core, chip = me % 2, me // 2
    orders = _orders(bits)
    width = block.shape[1]
    cur = block[None]
    for k in reversed(range(bits)):
        bit_here = (chip >> jnp.where(core == 0, orders[0][k], orders[1][k])) & 1
        partner = [(j, j ^ (2 << orders[j % 2][k])) for j in range(n)]
        got = lax.ppermute(cur, axis, partner)
        if k == 0:
            before = work(cur.reshape(-1, width))
        cur = _interleave(cur, got, bit_here)
    if bits:
        cur, before = lax.optimization_barrier((cur, before))
        after = work(got.reshape(-1, width))
    other = lax.ppermute(cur, axis, [(j, j ^ 1) for j in range(n)])
    if not bits:
        return work(block), other.reshape(-1, width)
    other, after = lax.optimization_barrier((other, after))
    shaped = lambda r: r.reshape(got.shape[0], block.shape[0], *r.shape[1:])
    done = [_interleave(shaped(b), shaped(a), bit_here) for b, a in zip(before, after)]
    return [d.reshape(-1, *d.shape[2:]) for d in done], other.reshape(-1, width)


def halving_rest(keep, send, axis):
    n = lax.axis_size(axis)
    chips = n // 2
    bits = chips.bit_length() - 1
    me = lax.axis_index(axis)
    core, chip = me % 2, me // 2
    got = lax.ppermute(send, axis, [(j, j ^ 1) for j in range(n)])
    cur = (keep + got.astype(jnp.float32)).reshape(chips, -1, keep.shape[-1])
    for t in range(bits):
        order = jnp.where(core == 0, t, _swap01(t, bits))
        bit_here = (chip >> order) & 1
        pairs = cur.reshape(cur.shape[0] // 2, 2, *cur.shape[1:])
        kept = lax.dynamic_index_in_dim(pairs, bit_here, axis=1, keepdims=False)
        sent = lax.dynamic_index_in_dim(pairs, 1 - bit_here, axis=1, keepdims=False)
        partner = [(j, j ^ (2 << (t if j % 2 == 0 else _swap01(t, bits)))) for j in range(n)]
        got = lax.ppermute(sent.astype(jnp.bfloat16), axis, partner)
        cur = kept + got.astype(jnp.float32)
    return cur[0]


def expert_hidden(packed, w_gate, w_up, model_width, experts, expert):
    rows = packed[:, :model_width]
    parts = packed[:, model_width:model_width + 3 * experts].astype(jnp.float32)
    parts = parts.reshape(-1, 3, experts)
    weight_all = parts[:, 0] + (parts[:, 1] + parts[:, 2])
    weight = jnp.sum(jnp.where(jnp.arange(experts)[None, :] == expert, weight_all, 0.0), axis=1)
    gate_act = jnp.dot(rows, w_gate, preferred_element_type=jnp.float32)
    up_act = jnp.dot(rows, w_up, preferred_element_type=jnp.float32)
    hidden = (jax.nn.silu(gate_act) * up_act).astype(jnp.bfloat16)
    return hidden, weight


def shards(moe_rows, routes, route_weights, w_gate, w_up, w_down, queries, latent_cache, lengths):
    attn_out = attend(queries, latent_cache, lengths)
    rows_here, model_width = moe_rows.shape
    experts = lax.axis_size("ep") // 2
    expert = lax.axis_index("ep") // 2
    named = routes[:, :, None] == jnp.arange(experts, dtype=jnp.int32)[None, None, :]
    dense_w = jnp.sum(jnp.where(named, route_weights[:, :, None], 0.0), axis=1)
    hi = lax.reduce_precision(dense_w, exponent_bits=8, mantissa_bits=7)
    rest = dense_w - hi
    mid = lax.reduce_precision(rest, exponent_bits=8, mantissa_bits=7)
    lo = rest - mid
    hi, mid, lo = (p.astype(jnp.bfloat16) for p in (hi, mid, lo))
    extra = -(-3 * experts // 128) * 128
    tail = jnp.zeros((rows_here, extra - 3 * experts), jnp.bfloat16)
    packed = jnp.concatenate([moe_rows, hi, mid, lo, tail], axis=1)
    args = (w_gate[0], w_up[0], model_width, experts, expert)
    (keep_hidden, keep_weight), other = doubling_gather(
        packed, "ep", lambda rows: expert_hidden(rows, *args)
    )
    send_hidden, send_weight = expert_hidden(other, *args)
    send = jnp.dot(send_hidden, w_down[0], preferred_element_type=jnp.float32)
    send = (send * send_weight[:, None]).astype(jnp.bfloat16)
    keep = jnp.dot(keep_hidden, w_down[0], preferred_element_type=jnp.float32)
    keep = keep * keep_weight[:, None]
    moe_out = halving_rest(keep, send, "ep")
    return (moe_out.astype(jnp.bfloat16), attn_out)


def solution(mesh):
    in_specs = (
        P(("dp", "ep"), None),
        P(("dp", "ep"), None),
        P(("dp", "ep"), None),
        P("ep", None, None),
        P("ep", None, None),
        P("ep", None, None),
        P(("dp", "ep"), None, None),
        P(("dp", "ep"), None, None),
        P(("dp", "ep")),
    )
    out_specs = (P(("dp", "ep"), None), P(("dp", "ep"), None, None))
    return jax.shard_map(shards, mesh=mesh, in_specs=in_specs, out_specs=out_specs, check_vma=False)
```

```python
import jax
import jax.numpy as jnp
from jax import lax
from jax.sharding import PartitionSpec as P

LATENT = 512


score_scale = 192.0 ** (-0.5)


def attend(queries, latent_cache, lengths):
    scores = (
        jnp.einsum("rhc,rlc->rhl", queries, latent_cache, preferred_element_type=jnp.float32)
        * score_scale
    )
    in_range = (
        jnp.arange(latent_cache.shape[1], dtype=jnp.int32)[None, None, :] < lengths[:, None, None]
    )
    scores = jnp.where(in_range, scores, -1e30)
    highest = jnp.max(scores, axis=-1, keepdims=True)
    expo = jnp.where(in_range, jnp.exp(scores - highest), 0.0)
    probs = (expo / jnp.sum(expo, axis=-1, keepdims=True)).astype(jnp.bfloat16)
    return jnp.einsum(
        "rhl,rlc->rhc", probs, latent_cache[:, :, :LATENT], preferred_element_type=jnp.float32
    ).astype(jnp.bfloat16)


def _swap01(t, bits):
    return {0: 1, 1: 0}.get(t, t) if bits > 1 else t


def _orders(bits):
    return [list(range(bits)), [_swap01(t, bits) for t in range(bits)]]


def _interleave(a, b, bit):
    pair = jnp.where(bit == 0, jnp.stack([a, b], axis=1), jnp.stack([b, a], axis=1))
    return pair.reshape(2 * a.shape[0], *a.shape[1:])


def doubling_gather(block, axis, work):
    n = lax.axis_size(axis)
    chips = n // 2
    bits = chips.bit_length() - 1
    me = lax.axis_index(axis)
    core, chip = me % 2, me // 2
    orders = _orders(bits)
    width = block.shape[1]
    cur = block[None]
    for k in reversed(range(bits)):
        bit_here = (chip >> jnp.where(core == 0, orders[0][k], orders[1][k])) & 1
        partner = [(j, j ^ (2 << orders[j % 2][k])) for j in range(n)]
        got = lax.ppermute(cur, axis, partner)
        if k == 0:
            before = work(cur.reshape(-1, width))
        cur = _interleave(cur, got, bit_here)
    if bits:
        cur, before = lax.optimization_barrier((cur, before))
        after = work(got.reshape(-1, width))
    other = lax.ppermute(cur, axis, [(j, j ^ 1) for j in range(n)])
    if not bits:
        return work(block), other.reshape(-1, width)
    other, after = lax.optimization_barrier((other, after))
    shaped = lambda r: r.reshape(got.shape[0], block.shape[0], *r.shape[1:])
    done = [_interleave(shaped(b), shaped(a), bit_here) for b, a in zip(before, after)]
    return [d.reshape(-1, *d.shape[2:]) for d in done], other.reshape(-1, width)


def halving_rest(keep, send, axis):
    n = lax.axis_size(axis)
    chips = n // 2
    bits = chips.bit_length() - 1
    me = lax.axis_index(axis)
    core, chip = me % 2, me // 2
    got = lax.ppermute(send, axis, [(j, j ^ 1) for j in range(n)])
    cur = (keep + got.astype(jnp.float32)).reshape(chips, -1, keep.shape[-1])
    for t in range(bits):
        order = jnp.where(core == 0, t, _swap01(t, bits))
        bit_here = (chip >> order) & 1
        pairs = cur.reshape(cur.shape[0] // 2, 2, *cur.shape[1:])
        kept = lax.dynamic_index_in_dim(pairs, bit_here, axis=1, keepdims=False)
        sent = lax.dynamic_index_in_dim(pairs, 1 - bit_here, axis=1, keepdims=False)
        partner = [(j, j ^ (2 << (t if j % 2 == 0 else _swap01(t, bits)))) for j in range(n)]
        got = lax.ppermute(sent.astype(jnp.bfloat16), axis, partner)
        cur = kept + got.astype(jnp.float32)
    return cur[0]


def expert_hidden(packed, w_gate, w_up, model_width, experts, expert):
    rows = packed[:, :model_width]
    parts = packed[:, model_width:model_width + 3 * experts].astype(jnp.float32)
    parts = parts.reshape(-1, 3, experts)
    weight_all = parts[:, 0] + (parts[:, 1] + parts[:, 2])
    weight = jnp.sum(jnp.where(jnp.arange(experts)[None, :] == expert, weight_all, 0.0), axis=1)
    gate_act = jnp.dot(rows, w_gate, preferred_element_type=jnp.float32)
    up_act = jnp.dot(rows, w_up, preferred_element_type=jnp.float32)
    hidden = (jax.nn.silu(gate_act) * up_act).astype(jnp.bfloat16)
    return hidden, weight


def shards(moe_rows, routes, route_weights, w_gate, w_up, w_down, queries, latent_cache, lengths):
    attn_out = attend(queries, latent_cache, lengths)
    rows_here, model_width = moe_rows.shape
    experts = lax.axis_size("ep") // 2
    expert = lax.axis_index("ep") // 2
    named = routes[:, :, None] == jnp.arange(experts, dtype=jnp.int32)[None, None, :]
    dense_w = jnp.sum(jnp.where(named, route_weights[:, :, None], 0.0), axis=1)
    hi = lax.reduce_precision(dense_w, exponent_bits=8, mantissa_bits=7)
    rest = dense_w - hi
    mid = lax.reduce_precision(rest, exponent_bits=8, mantissa_bits=7)
    lo = rest - mid
    hi, mid, lo = (p.astype(jnp.bfloat16) for p in (hi, mid, lo))
    extra = -(-3 * experts // 128) * 128
    tail = jnp.zeros((rows_here, extra - 3 * experts), jnp.bfloat16)
    packed = jnp.concatenate([moe_rows, hi, mid, lo, tail], axis=1)
    args = (w_gate[0], w_up[0], model_width, experts, expert)
    (keep_hidden, keep_weight), other = doubling_gather(
        packed, "ep", lambda rows: expert_hidden(rows, *args)
    )
    send_hidden, send_weight = expert_hidden(other, *args)
    send = jnp.dot(send_hidden, w_down[0], preferred_element_type=jnp.float32)
    send = (send * send_weight[:, None]).astype(jnp.bfloat16)
    keep = jnp.dot(keep_hidden, w_down[0], preferred_element_type=jnp.float32)
    keep = lax.optimization_barrier(keep * keep_weight[:, None])
    moe_out = halving_rest(keep, send, "ep")
    return (moe_out.astype(jnp.bfloat16), attn_out)


def solution(mesh):
    in_specs = (
        P(("dp", "ep"), None),
        P(("dp", "ep"), None),
        P(("dp", "ep"), None),
        P("ep", None, None),
        P("ep", None, None),
        P("ep", None, None),
        P(("dp", "ep"), None, None),
        P(("dp", "ep"), None, None),
        P(("dp", "ep")),
    )
    out_specs = (P(("dp", "ep"), None), P(("dp", "ep"), None, None))
    return jax.shard_map(shards, mesh=mesh, in_specs=in_specs, out_specs=out_specs, check_vma=False)
```

```python
import jax
import jax.numpy as jnp
from jax import lax
from jax.sharding import PartitionSpec as P

LATENT = 512


score_scale = 192.0 ** (-0.5)


def attend(queries, latent_cache, lengths):
    scores = (
        jnp.einsum("rhc,rlc->rhl", queries, latent_cache, preferred_element_type=jnp.float32)
        * score_scale
    )
    in_range = (
        jnp.arange(latent_cache.shape[1], dtype=jnp.int32)[None, None, :] < lengths[:, None, None]
    )
    scores = jnp.where(in_range, scores, -1e30)
    highest = jnp.max(scores, axis=-1, keepdims=True)
    expo = jnp.where(in_range, jnp.exp(scores - highest), 0.0)
    probs = (expo / jnp.sum(expo, axis=-1, keepdims=True)).astype(jnp.bfloat16)
    return jnp.einsum(
        "rhl,rlc->rhc", probs, latent_cache[:, :, :LATENT], preferred_element_type=jnp.float32
    ).astype(jnp.bfloat16)


def _swap01(t, bits):
    return {0: 1, 1: 0}.get(t, t) if bits > 1 else t


def _orders(bits):
    return [list(range(bits)), [_swap01(t, bits) for t in range(bits)]]


def _interleave(a, b, bit):
    pair = jnp.where(bit == 0, jnp.stack([a, b], axis=1), jnp.stack([b, a], axis=1))
    return pair.reshape(2 * a.shape[0], *a.shape[1:])


def doubling_gather(block, axis, work):
    n = lax.axis_size(axis)
    chips = n // 2
    bits = chips.bit_length() - 1
    me = lax.axis_index(axis)
    core, chip = me % 2, me // 2
    orders = _orders(bits)
    width = block.shape[1]
    cur = block[None]
    for k in reversed(range(bits)):
        bit_here = (chip >> jnp.where(core == 0, orders[0][k], orders[1][k])) & 1
        partner = [(j, j ^ (2 << orders[j % 2][k])) for j in range(n)]
        got = lax.ppermute(cur, axis, partner)
        if k == 0:
            before = work(cur.reshape(-1, width))
        cur = _interleave(cur, got, bit_here)
    if bits:
        cur, before = lax.optimization_barrier((cur, before))
        after = work(got.reshape(-1, width))
    other = lax.ppermute(cur, axis, [(j, j ^ 1) for j in range(n)])
    if not bits:
        return work(block), other.reshape(-1, width)
    other, after = lax.optimization_barrier((other, after))
    shaped = lambda r: r.reshape(got.shape[0], block.shape[0], *r.shape[1:])
    done = [_interleave(shaped(b), shaped(a), bit_here) for b, a in zip(before, after)]
    return [d.reshape(-1, *d.shape[2:]) for d in done], other.reshape(-1, width)


def halving_rest(keep, send, axis):
    n = lax.axis_size(axis)
    chips = n // 2
    bits = chips.bit_length() - 1
    me = lax.axis_index(axis)
    core, chip = me % 2, me // 2
    got = lax.ppermute(send, axis, [(j, j ^ 1) for j in range(n)])
    cur = (keep + got.astype(jnp.float32)).reshape(chips, -1, keep.shape[-1])
    for t in range(bits):
        order = jnp.where(core == 0, t, _swap01(t, bits))
        bit_here = (chip >> order) & 1
        pairs = cur.reshape(cur.shape[0] // 2, 2, *cur.shape[1:])
        kept = lax.dynamic_index_in_dim(pairs, bit_here, axis=1, keepdims=False)
        sent = lax.dynamic_index_in_dim(pairs, 1 - bit_here, axis=1, keepdims=False)
        partner = [(j, j ^ (2 << (t if j % 2 == 0 else _swap01(t, bits)))) for j in range(n)]
        got = lax.ppermute(sent.astype(jnp.bfloat16), axis, partner)
        cur = kept + got.astype(jnp.float32)
    return cur[0]


def expert_hidden(packed, w_gate, w_up, model_width, experts, expert):
    rows = packed[:, :model_width]
    parts = packed[:, model_width:model_width + 3 * experts].astype(jnp.float32)
    parts = parts.reshape(-1, 3, experts)
    weight_all = parts[:, 0] + (parts[:, 1] + parts[:, 2])
    weight = jnp.sum(jnp.where(jnp.arange(experts)[None, :] == expert, weight_all, 0.0), axis=1)
    gate_act = jnp.dot(rows, w_gate, preferred_element_type=jnp.float32)
    up_act = jnp.dot(rows, w_up, preferred_element_type=jnp.float32)
    hidden = (jax.nn.silu(gate_act) * up_act).astype(jnp.bfloat16)
    return hidden, weight


def shards(moe_rows, routes, route_weights, w_gate, w_up, w_down, queries, latent_cache, lengths):
    attn_out = attend(queries, latent_cache, lengths)
    rows_here, model_width = moe_rows.shape
    experts = lax.axis_size("ep") // 2
    expert = lax.axis_index("ep") // 2
    named = routes[:, :, None] == jnp.arange(experts, dtype=jnp.int32)[None, None, :]
    dense_w = jnp.sum(jnp.where(named, route_weights[:, :, None], 0.0), axis=1)
    hi = lax.reduce_precision(dense_w, exponent_bits=8, mantissa_bits=7)
    rest = dense_w - hi
    mid = lax.reduce_precision(rest, exponent_bits=8, mantissa_bits=7)
    lo = rest - mid
    hi, mid, lo = (p.astype(jnp.bfloat16) for p in (hi, mid, lo))
    extra = -(-3 * experts // 128) * 128
    tail = jnp.zeros((rows_here, extra - 3 * experts), jnp.bfloat16)
    packed = jnp.concatenate([moe_rows, hi, mid, lo, tail], axis=1)
    args = (w_gate[0], w_up[0], model_width, experts, expert)
    (keep_hidden, keep_weight), other = doubling_gather(
        packed, "ep", lambda rows: expert_hidden(rows, *args)
    )
    send_hidden, send_weight = expert_hidden(other, *args)
    send = jnp.dot(send_hidden, w_down[0], preferred_element_type=jnp.float32)
    send = (send * send_weight[:, None]).astype(jnp.bfloat16)
    keep = jnp.dot(keep_hidden, w_down[0], preferred_element_type=jnp.float32)
    keep = lax.optimization_barrier(keep * keep_weight[:, None])
    half = model_width // 2
    moe_out = jnp.concatenate(
        [halving_rest(keep[:, :half], send[:, :half], "ep"), halving_rest(keep[:, half:], send[:, half:], "ep")],
        axis=1,
    )
    return (moe_out.astype(jnp.bfloat16), attn_out)


def solution(mesh):
    in_specs = (
        P(("dp", "ep"), None),
        P(("dp", "ep"), None),
        P(("dp", "ep"), None),
        P("ep", None, None),
        P("ep", None, None),
        P("ep", None, None),
        P(("dp", "ep"), None, None),
        P(("dp", "ep"), None, None),
        P(("dp", "ep")),
    )
    out_specs = (P(("dp", "ep"), None), P(("dp", "ep"), None, None))
    return jax.shard_map(shards, mesh=mesh, in_specs=in_specs, out_specs=out_specs, check_vma=False)
```

```python
import jax
import jax.numpy as jnp
from jax import lax
from jax.sharding import PartitionSpec as P

LATENT = 512


score_scale = 192.0 ** (-0.5)


def attend(queries, latent_cache, lengths):
    scores = (
        jnp.einsum("rhc,rlc->rhl", queries, latent_cache, preferred_element_type=jnp.float32)
        * score_scale
    )
    in_range = (
        jnp.arange(latent_cache.shape[1], dtype=jnp.int32)[None, None, :] < lengths[:, None, None]
    )
    scores = jnp.where(in_range, scores, -1e30)
    highest = jnp.max(scores, axis=-1, keepdims=True)
    expo = jnp.where(in_range, jnp.exp(scores - highest), 0.0)
    probs = (expo / jnp.sum(expo, axis=-1, keepdims=True)).astype(jnp.bfloat16)
    return jnp.einsum(
        "rhl,rlc->rhc", probs, latent_cache[:, :, :LATENT], preferred_element_type=jnp.float32
    ).astype(jnp.bfloat16)


def _swap01(t, bits):
    return {0: 1, 1: 0}.get(t, t) if bits > 1 else t


def _orders(bits):
    return [list(range(bits)), [_swap01(t, bits) for t in range(bits)]]


def _interleave(a, b, bit):
    pair = jnp.where(bit == 0, jnp.stack([a, b], axis=1), jnp.stack([b, a], axis=1))
    return pair.reshape(2 * a.shape[0], *a.shape[1:])


def doubling_gather(block, axis, work, companion):
    n = lax.axis_size(axis)
    chips = n // 2
    bits = chips.bit_length() - 1
    me = lax.axis_index(axis)
    core, chip = me % 2, me // 2
    orders = _orders(bits)
    width = block.shape[1]
    cur = block[None]
    for k in reversed(range(bits)):
        bit_here = (chip >> jnp.where(core == 0, orders[0][k], orders[1][k])) & 1
        partner = [(j, j ^ (2 << orders[j % 2][k])) for j in range(n)]
        got = lax.ppermute(cur, axis, partner)
        if k == bits - 1:
            got, companion = lax.optimization_barrier((got, companion))
        if k == 0:
            before = work(cur.reshape(-1, width))
        cur = _interleave(cur, got, bit_here)
    if bits:
        cur, before = lax.optimization_barrier((cur, before))
        after = work(got.reshape(-1, width))
    other = lax.ppermute(cur, axis, [(j, j ^ 1) for j in range(n)])
    if not bits:
        return work(block), other.reshape(-1, width), companion
    other, after = lax.optimization_barrier((other, after))
    shaped = lambda r: r.reshape(got.shape[0], block.shape[0], *r.shape[1:])
    done = [_interleave(shaped(b), shaped(a), bit_here) for b, a in zip(before, after)]
    return [d.reshape(-1, *d.shape[2:]) for d in done], other.reshape(-1, width), companion


def halving_rest(keep, send, axis):
    n = lax.axis_size(axis)
    chips = n // 2
    bits = chips.bit_length() - 1
    me = lax.axis_index(axis)
    core, chip = me % 2, me // 2
    got = lax.ppermute(send, axis, [(j, j ^ 1) for j in range(n)])
    cur = (keep + got.astype(jnp.float32)).reshape(chips, -1, keep.shape[-1])
    for t in range(bits):
        order = jnp.where(core == 0, t, _swap01(t, bits))
        bit_here = (chip >> order) & 1
        pairs = cur.reshape(cur.shape[0] // 2, 2, *cur.shape[1:])
        kept = lax.dynamic_index_in_dim(pairs, bit_here, axis=1, keepdims=False)
        sent = lax.dynamic_index_in_dim(pairs, 1 - bit_here, axis=1, keepdims=False)
        partner = [(j, j ^ (2 << (t if j % 2 == 0 else _swap01(t, bits)))) for j in range(n)]
        got = lax.ppermute(sent.astype(jnp.bfloat16), axis, partner)
        cur = kept + got.astype(jnp.float32)
    return cur[0]


def expert_hidden(packed, w_gate, w_up, model_width, experts, expert):
    rows = packed[:, :model_width]
    parts = packed[:, model_width:model_width + 3 * experts].astype(jnp.float32)
    parts = parts.reshape(-1, 3, experts)
    weight_all = parts[:, 0] + (parts[:, 1] + parts[:, 2])
    weight = jnp.sum(jnp.where(jnp.arange(experts)[None, :] == expert, weight_all, 0.0), axis=1)
    gate_act = jnp.dot(rows, w_gate, preferred_element_type=jnp.float32)
    up_act = jnp.dot(rows, w_up, preferred_element_type=jnp.float32)
    hidden = (jax.nn.silu(gate_act) * up_act).astype(jnp.bfloat16)
    return hidden, weight


def shards(moe_rows, routes, route_weights, w_gate, w_up, w_down, queries, latent_cache, lengths):
    attn_out = attend(queries, latent_cache, lengths)
    rows_here, model_width = moe_rows.shape
    experts = lax.axis_size("ep") // 2
    expert = lax.axis_index("ep") // 2
    named = routes[:, :, None] == jnp.arange(experts, dtype=jnp.int32)[None, None, :]
    dense_w = jnp.sum(jnp.where(named, route_weights[:, :, None], 0.0), axis=1)
    hi = lax.reduce_precision(dense_w, exponent_bits=8, mantissa_bits=7)
    rest = dense_w - hi
    mid = lax.reduce_precision(rest, exponent_bits=8, mantissa_bits=7)
    lo = rest - mid
    hi, mid, lo = (p.astype(jnp.bfloat16) for p in (hi, mid, lo))
    extra = -(-3 * experts // 128) * 128
    tail = jnp.zeros((rows_here, extra - 3 * experts), jnp.bfloat16)
    packed = jnp.concatenate([moe_rows, hi, mid, lo, tail], axis=1)
    args = (w_gate[0], w_up[0], model_width, experts, expert)
    (keep_hidden, keep_weight), other, attn_out = doubling_gather(
        packed, "ep", lambda rows: expert_hidden(rows, *args), attn_out
    )
    send_hidden, send_weight = expert_hidden(other, *args)
    send = jnp.dot(send_hidden, w_down[0], preferred_element_type=jnp.float32)
    send = (send * send_weight[:, None]).astype(jnp.bfloat16)
    keep = jnp.dot(keep_hidden, w_down[0], preferred_element_type=jnp.float32)
    keep = lax.optimization_barrier(keep * keep_weight[:, None])
    half = model_width // 2
    moe_out = jnp.concatenate(
        [halving_rest(keep[:, :half], send[:, :half], "ep"), halving_rest(keep[:, half:], send[:, half:], "ep")],
        axis=1,
    )
    return (moe_out.astype(jnp.bfloat16), attn_out)


def solution(mesh):
    in_specs = (
        P(("dp", "ep"), None),
        P(("dp", "ep"), None),
        P(("dp", "ep"), None),
        P("ep", None, None),
        P("ep", None, None),
        P("ep", None, None),
        P(("dp", "ep"), None, None),
        P(("dp", "ep"), None, None),
        P(("dp", "ep")),
    )
    out_specs = (P(("dp", "ep"), None), P(("dp", "ep"), None, None))
    return jax.shard_map(shards, mesh=mesh, in_specs=in_specs, out_specs=out_specs, check_vma=False)
```

```python
import jax
import jax.numpy as jnp
from jax import lax
from jax.sharding import PartitionSpec as P

LATENT = 512


score_scale = 192.0 ** (-0.5)


def attend(queries, latent_cache, lengths):
    scores = (
        jnp.einsum("rhc,rlc->rhl", queries, latent_cache, preferred_element_type=jnp.float32)
        * score_scale
    )
    in_range = (
        jnp.arange(latent_cache.shape[1], dtype=jnp.int32)[None, None, :] < lengths[:, None, None]
    )
    scores = jnp.where(in_range, scores, -1e30)
    highest = jnp.max(scores, axis=-1, keepdims=True)
    expo = jnp.where(in_range, jnp.exp(scores - highest), 0.0)
    probs = (expo / jnp.sum(expo, axis=-1, keepdims=True)).astype(jnp.bfloat16)
    return jnp.einsum(
        "rhl,rlc->rhc", probs, latent_cache[:, :, :LATENT], preferred_element_type=jnp.float32
    ).astype(jnp.bfloat16)


def _swap01(t, bits):
    return {0: 1, 1: 0}.get(t, t) if bits > 1 else t


def _orders(bits):
    return [list(range(bits)), [_swap01(t, bits) for t in range(bits)]]


def _interleave(a, b, bit):
    pair = jnp.where(bit == 0, jnp.stack([a, b], axis=1), jnp.stack([b, a], axis=1))
    return pair.reshape(2 * a.shape[0], *a.shape[1:])


def doubling_gather(block, axis, work, companion):
    n = lax.axis_size(axis)
    chips = n // 2
    bits = chips.bit_length() - 1
    me = lax.axis_index(axis)
    core, chip = me % 2, me // 2
    orders = _orders(bits)
    width = block.shape[1]
    cur = block[None]
    for k in reversed(range(bits)):
        bit_here = (chip >> jnp.where(core == 0, orders[0][k], orders[1][k])) & 1
        partner = [(j, j ^ (2 << orders[j % 2][k])) for j in range(n)]
        got = lax.ppermute(cur, axis, partner)
        if k == bits - 1:
            got, companion = lax.optimization_barrier((got, companion))
        if k == 0:
            before = work(cur.reshape(-1, width))
        cur = _interleave(cur, got, bit_here)
    if bits:
        cur, before = lax.optimization_barrier((cur, before))
        after = work(got.reshape(-1, width))
    other = lax.ppermute(cur, axis, [(j, j ^ 1) for j in range(n)])
    if not bits:
        return work(block), other.reshape(-1, width), companion
    other, after = lax.optimization_barrier((other, after))
    shaped = lambda r: r.reshape(got.shape[0], block.shape[0], *r.shape[1:])
    done = [_interleave(shaped(b), shaped(a), bit_here) for b, a in zip(before, after)]
    return [d.reshape(-1, *d.shape[2:]) for d in done], other.reshape(-1, width), companion


def halving_rest(keep, send, axis, chains=2):
    n = lax.axis_size(axis)
    chips = n // 2
    bits = chips.bit_length() - 1
    me = lax.axis_index(axis)
    core, chip = me % 2, me // 2
    got = lax.ppermute(send, axis, [(j, j ^ 1) for j in range(n)])
    total = (keep + got.astype(jnp.float32)).reshape(chips, -1, keep.shape[-1])
    outs = []
    for cur in jnp.split(total, chains, axis=2):
        for t in range(bits):
            order = jnp.where(core == 0, t, _swap01(t, bits))
            bit_here = (chip >> order) & 1
            pairs = cur.reshape(cur.shape[0] // 2, 2, *cur.shape[1:])
            kept = lax.dynamic_index_in_dim(pairs, bit_here, axis=1, keepdims=False)
            sent = lax.dynamic_index_in_dim(pairs, 1 - bit_here, axis=1, keepdims=False)
            partner = [(j, j ^ (2 << (t if j % 2 == 0 else _swap01(t, bits)))) for j in range(n)]
            got = lax.ppermute(sent.astype(jnp.bfloat16), axis, partner)
            cur = kept + got.astype(jnp.float32)
        outs.append(cur[0])
    return jnp.concatenate(outs, axis=1)


def expert_hidden(packed, w_gate, w_up, model_width, experts, expert):
    rows = packed[:, :model_width]
    parts = packed[:, model_width:model_width + 3 * experts].astype(jnp.float32)
    parts = parts.reshape(-1, 3, experts)
    weight_all = parts[:, 0] + (parts[:, 1] + parts[:, 2])
    weight = jnp.sum(jnp.where(jnp.arange(experts)[None, :] == expert, weight_all, 0.0), axis=1)
    gate_act = jnp.dot(rows, w_gate, preferred_element_type=jnp.float32)
    up_act = jnp.dot(rows, w_up, preferred_element_type=jnp.float32)
    hidden = (jax.nn.silu(gate_act) * up_act).astype(jnp.bfloat16)
    return hidden, weight


def shards(moe_rows, routes, route_weights, w_gate, w_up, w_down, queries, latent_cache, lengths):
    attn_out = attend(queries, latent_cache, lengths)
    rows_here, model_width = moe_rows.shape
    experts = lax.axis_size("ep") // 2
    expert = lax.axis_index("ep") // 2
    named = routes[:, :, None] == jnp.arange(experts, dtype=jnp.int32)[None, None, :]
    dense_w = jnp.sum(jnp.where(named, route_weights[:, :, None], 0.0), axis=1)
    hi = lax.reduce_precision(dense_w, exponent_bits=8, mantissa_bits=7)
    rest = dense_w - hi
    mid = lax.reduce_precision(rest, exponent_bits=8, mantissa_bits=7)
    lo = rest - mid
    hi, mid, lo = (p.astype(jnp.bfloat16) for p in (hi, mid, lo))
    extra = -(-3 * experts // 128) * 128
    tail = jnp.zeros((rows_here, extra - 3 * experts), jnp.bfloat16)
    packed = jnp.concatenate([moe_rows, hi, mid, lo, tail], axis=1)
    args = (w_gate[0], w_up[0], model_width, experts, expert)
    (keep_hidden, keep_weight), other, attn_out = doubling_gather(
        packed, "ep", lambda rows: expert_hidden(rows, *args), attn_out
    )
    send_hidden, send_weight = expert_hidden(other, *args)
    send = jnp.dot(send_hidden, w_down[0], preferred_element_type=jnp.float32)
    send = (send * send_weight[:, None]).astype(jnp.bfloat16)
    keep = jnp.dot(keep_hidden, w_down[0], preferred_element_type=jnp.float32)
    keep = lax.optimization_barrier(keep * keep_weight[:, None])
    moe_out = halving_rest(keep, send, "ep")
    return (moe_out.astype(jnp.bfloat16), attn_out)


def solution(mesh):
    in_specs = (
        P(("dp", "ep"), None),
        P(("dp", "ep"), None),
        P(("dp", "ep"), None),
        P("ep", None, None),
        P("ep", None, None),
        P("ep", None, None),
        P(("dp", "ep"), None, None),
        P(("dp", "ep"), None, None),
        P(("dp", "ep")),
    )
    out_specs = (P(("dp", "ep"), None), P(("dp", "ep"), None, None))
    return jax.shard_map(shards, mesh=mesh, in_specs=in_specs, out_specs=out_specs, check_vma=False)
```

```python
import jax
import jax.numpy as jnp
from jax import lax
from jax.sharding import PartitionSpec as P

LATENT = 512


score_scale = 192.0 ** (-0.5)


def attend(queries, latent_cache, lengths):
    scores = (
        jnp.einsum("rhc,rlc->rhl", queries, latent_cache, preferred_element_type=jnp.float32)
        * score_scale
    )
    in_range = (
        jnp.arange(latent_cache.shape[1], dtype=jnp.int32)[None, None, :] < lengths[:, None, None]
    )
    scores = jnp.where(in_range, scores, -1e30)
    highest = jnp.max(scores, axis=-1, keepdims=True)
    expo = jnp.where(in_range, jnp.exp(scores - highest), 0.0)
    probs = (expo / jnp.sum(expo, axis=-1, keepdims=True)).astype(jnp.bfloat16)
    return jnp.einsum(
        "rhl,rlc->rhc", probs, latent_cache[:, :, :LATENT], preferred_element_type=jnp.float32
    ).astype(jnp.bfloat16)


def _swap01(t, bits):
    return {0: 1, 1: 0}.get(t, t) if bits > 1 else t


def _orders(bits):
    return [list(range(bits)), [_swap01(t, bits) for t in range(bits)]]


def _interleave(a, b, bit):
    pair = jnp.where(bit == 0, jnp.stack([a, b], axis=1), jnp.stack([b, a], axis=1))
    return pair.reshape(2 * a.shape[0], *a.shape[1:])


def doubling_gather(block, axis, work, companion):
    n = lax.axis_size(axis)
    chips = n // 2
    bits = chips.bit_length() - 1
    me = lax.axis_index(axis)
    core, chip = me % 2, me // 2
    orders = _orders(bits)
    width = block.shape[1]
    cur = block[None]
    for k in reversed(range(bits)):
        bit_here = (chip >> jnp.where(core == 0, orders[0][k], orders[1][k])) & 1
        partner = [(j, j ^ (2 << orders[j % 2][k])) for j in range(n)]
        got = lax.ppermute(cur, axis, partner)
        if k == bits - 1:
            got, companion = lax.optimization_barrier((got, companion))
        if k == 0:
            before = work(cur.reshape(-1, width))
        cur = _interleave(cur, got, bit_here)
    if bits:
        cur, before = lax.optimization_barrier((cur, before))
        after = work(got.reshape(-1, width))
    other = lax.ppermute(cur, axis, [(j, j ^ 1) for j in range(n)])
    if not bits:
        return work(block), other.reshape(-1, width), companion
    other, after = lax.optimization_barrier((other, after))
    shaped = lambda r: r.reshape(got.shape[0], block.shape[0], *r.shape[1:])
    done = [_interleave(shaped(b), shaped(a), bit_here) for b, a in zip(before, after)]
    return [d.reshape(-1, *d.shape[2:]) for d in done], other.reshape(-1, width), companion


def halving_rest(keep, send, axis, chains=4):
    n = lax.axis_size(axis)
    chips = n // 2
    bits = chips.bit_length() - 1
    me = lax.axis_index(axis)
    core, chip = me % 2, me // 2
    got = lax.ppermute(send, axis, [(j, j ^ 1) for j in range(n)])
    total = (keep + got.astype(jnp.float32)).reshape(chips, -1, keep.shape[-1])
    outs = []
    for cur in jnp.split(total, chains, axis=2):
        for t in range(bits):
            order = jnp.where(core == 0, t, _swap01(t, bits))
            bit_here = (chip >> order) & 1
            pairs = cur.reshape(cur.shape[0] // 2, 2, *cur.shape[1:])
            kept = lax.dynamic_index_in_dim(pairs, bit_here, axis=1, keepdims=False)
            sent = lax.dynamic_index_in_dim(pairs, 1 - bit_here, axis=1, keepdims=False)
            partner = [(j, j ^ (2 << (t if j % 2 == 0 else _swap01(t, bits)))) for j in range(n)]
            got = lax.ppermute(sent.astype(jnp.bfloat16), axis, partner)
            cur = kept + got.astype(jnp.float32)
        outs.append(cur[0])
    return jnp.concatenate(outs, axis=1)


def expert_hidden(packed, w_gate, w_up, model_width, experts, expert):
    rows = packed[:, :model_width]
    parts = packed[:, model_width:model_width + 3 * experts].astype(jnp.float32)
    parts = parts.reshape(-1, 3, experts)
    weight_all = parts[:, 0] + (parts[:, 1] + parts[:, 2])
    weight = jnp.sum(jnp.where(jnp.arange(experts)[None, :] == expert, weight_all, 0.0), axis=1)
    gate_act = jnp.dot(rows, w_gate, preferred_element_type=jnp.float32)
    up_act = jnp.dot(rows, w_up, preferred_element_type=jnp.float32)
    hidden = (jax.nn.silu(gate_act) * up_act).astype(jnp.bfloat16)
    return hidden, weight


def shards(moe_rows, routes, route_weights, w_gate, w_up, w_down, queries, latent_cache, lengths):
    attn_out = attend(queries, latent_cache, lengths)
    rows_here, model_width = moe_rows.shape
    experts = lax.axis_size("ep") // 2
    expert = lax.axis_index("ep") // 2
    named = routes[:, :, None] == jnp.arange(experts, dtype=jnp.int32)[None, None, :]
    dense_w = jnp.sum(jnp.where(named, route_weights[:, :, None], 0.0), axis=1)
    hi = lax.reduce_precision(dense_w, exponent_bits=8, mantissa_bits=7)
    rest = dense_w - hi
    mid = lax.reduce_precision(rest, exponent_bits=8, mantissa_bits=7)
    lo = rest - mid
    hi, mid, lo = (p.astype(jnp.bfloat16) for p in (hi, mid, lo))
    extra = -(-3 * experts // 128) * 128
    tail = jnp.zeros((rows_here, extra - 3 * experts), jnp.bfloat16)
    packed = jnp.concatenate([moe_rows, hi, mid, lo, tail], axis=1)
    args = (w_gate[0], w_up[0], model_width, experts, expert)
    (keep_hidden, keep_weight), other, attn_out = doubling_gather(
        packed, "ep", lambda rows: expert_hidden(rows, *args), attn_out
    )
    send_hidden, send_weight = expert_hidden(other, *args)
    send = jnp.dot(send_hidden, w_down[0], preferred_element_type=jnp.float32)
    send = (send * send_weight[:, None]).astype(jnp.bfloat16)
    keep = jnp.dot(keep_hidden, w_down[0], preferred_element_type=jnp.float32)
    keep = lax.optimization_barrier(keep * keep_weight[:, None])
    moe_out = halving_rest(keep, send, "ep")
    return (moe_out.astype(jnp.bfloat16), attn_out)


def solution(mesh):
    in_specs = (
        P(("dp", "ep"), None),
        P(("dp", "ep"), None),
        P(("dp", "ep"), None),
        P("ep", None, None),
        P("ep", None, None),
        P("ep", None, None),
        P(("dp", "ep"), None, None),
        P(("dp", "ep"), None, None),
        P(("dp", "ep")),
    )
    out_specs = (P(("dp", "ep"), None), P(("dp", "ep"), None, None))
    return jax.shard_map(shards, mesh=mesh, in_specs=in_specs, out_specs=out_specs, check_vma=False)
```

```python
import jax
import jax.numpy as jnp
from jax import lax
from jax.sharding import PartitionSpec as P

LATENT = 512


score_scale = 192.0 ** (-0.5)


def attend(queries, latent_cache, lengths):
    scores = (
        jnp.einsum("rhc,rlc->rhl", queries, latent_cache, preferred_element_type=jnp.float32)
        * score_scale
    )
    in_range = (
        jnp.arange(latent_cache.shape[1], dtype=jnp.int32)[None, None, :] < lengths[:, None, None]
    )
    scores = jnp.where(in_range, scores, -1e30)
    highest = jnp.max(scores, axis=-1, keepdims=True)
    expo = jnp.where(in_range, jnp.exp(scores - highest), 0.0)
    probs = (expo / jnp.sum(expo, axis=-1, keepdims=True)).astype(jnp.bfloat16)
    return jnp.einsum(
        "rhl,rlc->rhc", probs, latent_cache[:, :, :LATENT], preferred_element_type=jnp.float32
    ).astype(jnp.bfloat16)


def _swap01(t, bits):
    return {0: 1, 1: 0}.get(t, t) if bits > 1 else t


def _orders(bits):
    return [list(range(bits)), [_swap01(t, bits) for t in range(bits)]]


def _interleave(a, b, bit):
    pair = jnp.where(bit == 0, jnp.stack([a, b], axis=1), jnp.stack([b, a], axis=1))
    return pair.reshape(2 * a.shape[0], *a.shape[1:])


def doubling_gather(block, axis, near, far, companion):
    n = lax.axis_size(axis)
    chips = n // 2
    bits = chips.bit_length() - 1
    me = lax.axis_index(axis)
    core, chip = me % 2, me // 2
    orders = _orders(bits)
    width = block.shape[1]
    swap = [(j, j ^ 1) for j in range(n)]
    if not bits:
        return near(block), far(lax.ppermute(block, axis, swap)), companion
    cur = block[None]
    for k in reversed(range(bits)):
        bit_here = (chip >> jnp.where(core == 0, orders[0][k], orders[1][k])) & 1
        partner = [(j, j ^ (2 << orders[j % 2][k])) for j in range(n)]
        got = lax.ppermute(cur, axis, partner)
        if k == bits - 1:
            got, companion = lax.optimization_barrier((got, companion))
        if k == 0:
            before = near(cur.reshape(-1, width))
            early = far(lax.ppermute(cur, axis, swap).reshape(-1, width))
        cur = _interleave(cur, got, bit_here)
    got, before, early = lax.optimization_barrier((got, before, early))
    after = near(got.reshape(-1, width))
    late = lax.ppermute(got, axis, swap)
    late, after = lax.optimization_barrier((late, after))
    late = far(late.reshape(-1, width))
    bit_there = (chip >> jnp.where(core == 0, orders[1][0], orders[0][0])) & 1
    shaped = lambda r: r.reshape(got.shape[0], block.shape[0], *r.shape[1:])
    mine = [_interleave(shaped(b), shaped(a), bit_here) for b, a in zip(before, after)]
    theirs = [_interleave(shaped(e), shaped(l), bit_there) for e, l in zip(early, late)]
    flat = lambda parts: [d.reshape(-1, *d.shape[2:]) for d in parts]
    return flat(mine), flat(theirs), companion


def halving_rest(keep, send, axis, chains=2):
    n = lax.axis_size(axis)
    chips = n // 2
    bits = chips.bit_length() - 1
    me = lax.axis_index(axis)
    core, chip = me % 2, me // 2
    got = lax.ppermute(send, axis, [(j, j ^ 1) for j in range(n)])
    total = (keep + got.astype(jnp.float32)).reshape(chips, -1, keep.shape[-1])
    outs = []
    for cur in jnp.split(total, chains, axis=2):
        for t in range(bits):
            order = jnp.where(core == 0, t, _swap01(t, bits))
            bit_here = (chip >> order) & 1
            pairs = cur.reshape(cur.shape[0] // 2, 2, *cur.shape[1:])
            kept = lax.dynamic_index_in_dim(pairs, bit_here, axis=1, keepdims=False)
            sent = lax.dynamic_index_in_dim(pairs, 1 - bit_here, axis=1, keepdims=False)
            partner = [(j, j ^ (2 << (t if j % 2 == 0 else _swap01(t, bits)))) for j in range(n)]
            got = lax.ppermute(sent.astype(jnp.bfloat16), axis, partner)
            cur = kept + got.astype(jnp.float32)
        outs.append(cur[0])
    return jnp.concatenate(outs, axis=1)


def expert_hidden(packed, w_gate, w_up, model_width, experts, expert):
    rows = packed[:, :model_width]
    parts = packed[:, model_width:model_width + 3 * experts].astype(jnp.float32)
    parts = parts.reshape(-1, 3, experts)
    weight_all = parts[:, 0] + (parts[:, 1] + parts[:, 2])
    weight = jnp.sum(jnp.where(jnp.arange(experts)[None, :] == expert, weight_all, 0.0), axis=1)
    gate_act = jnp.dot(rows, w_gate, preferred_element_type=jnp.float32)
    up_act = jnp.dot(rows, w_up, preferred_element_type=jnp.float32)
    hidden = (jax.nn.silu(gate_act) * up_act).astype(jnp.bfloat16)
    return hidden, weight


def shards(moe_rows, routes, route_weights, w_gate, w_up, w_down, queries, latent_cache, lengths):
    attn_out = attend(queries, latent_cache, lengths)
    rows_here, model_width = moe_rows.shape
    experts = lax.axis_size("ep") // 2
    expert = lax.axis_index("ep") // 2
    named = routes[:, :, None] == jnp.arange(experts, dtype=jnp.int32)[None, None, :]
    dense_w = jnp.sum(jnp.where(named, route_weights[:, :, None], 0.0), axis=1)
    hi = lax.reduce_precision(dense_w, exponent_bits=8, mantissa_bits=7)
    rest = dense_w - hi
    mid = lax.reduce_precision(rest, exponent_bits=8, mantissa_bits=7)
    lo = rest - mid
    hi, mid, lo = (p.astype(jnp.bfloat16) for p in (hi, mid, lo))
    extra = -(-3 * experts // 128) * 128
    tail = jnp.zeros((rows_here, extra - 3 * experts), jnp.bfloat16)
    packed = jnp.concatenate([moe_rows, hi, mid, lo, tail], axis=1)
    args = (w_gate[0], w_up[0], model_width, experts, expert)

    def sent_out(rows):
        hidden, weight = expert_hidden(rows, *args)
        out = jnp.dot(hidden, w_down[0], preferred_element_type=jnp.float32)
        return ((out * weight[:, None]).astype(jnp.bfloat16),)

    (keep_hidden, keep_weight), (send,), attn_out = doubling_gather(
        packed, "ep", lambda rows: expert_hidden(rows, *args), sent_out, attn_out
    )
    keep = jnp.dot(keep_hidden, w_down[0], preferred_element_type=jnp.float32)
    keep = lax.optimization_barrier(keep * keep_weight[:, None])
    moe_out = halving_rest(keep, send, "ep")
    return (moe_out.astype(jnp.bfloat16), attn_out)


def solution(mesh):
    in_specs = (
        P(("dp", "ep"), None),
        P(("dp", "ep"), None),
        P(("dp", "ep"), None),
        P("ep", None, None),
        P("ep", None, None),
        P("ep", None, None),
        P(("dp", "ep"), None, None),
        P(("dp", "ep"), None, None),
        P(("dp", "ep")),
    )
    out_specs = (P(("dp", "ep"), None), P(("dp", "ep"), None, None))
    return jax.shard_map(shards, mesh=mesh, in_specs=in_specs, out_specs=out_specs, check_vma=False)
```

```python
import jax
import jax.numpy as jnp
from jax import lax
from jax.sharding import PartitionSpec as P

LATENT = 512


score_scale = 192.0 ** (-0.5)


def attend(queries, latent_cache, lengths):
    scores = (
        jnp.einsum("rhc,rlc->rhl", queries, latent_cache, preferred_element_type=jnp.float32)
        * score_scale
    )
    in_range = (
        jnp.arange(latent_cache.shape[1], dtype=jnp.int32)[None, None, :] < lengths[:, None, None]
    )
    scores = jnp.where(in_range, scores, -1e30)
    highest = jnp.max(scores, axis=-1, keepdims=True)
    expo = jnp.where(in_range, jnp.exp(scores - highest), 0.0)
    probs = (expo / jnp.sum(expo, axis=-1, keepdims=True)).astype(jnp.bfloat16)
    return jnp.einsum(
        "rhl,rlc->rhc", probs, latent_cache[:, :, :LATENT], preferred_element_type=jnp.float32
    ).astype(jnp.bfloat16)


def _swap01(t, bits):
    return {0: 1, 1: 0}.get(t, t) if bits > 1 else t


def _orders(bits):
    return [list(range(bits)), [_swap01(t, bits) for t in range(bits)]]


def _interleave(a, b, bit):
    pair = jnp.where(bit == 0, jnp.stack([a, b], axis=1), jnp.stack([b, a], axis=1))
    return pair.reshape(2 * a.shape[0], *a.shape[1:])


def doubling_gather(block, axis, work, companion):
    n = lax.axis_size(axis)
    chips = n // 2
    bits = chips.bit_length() - 1
    me = lax.axis_index(axis)
    core, chip = me % 2, me // 2
    orders = _orders(bits)
    width = block.shape[1]
    cur = block[None]
    for k in reversed(range(bits)):
        bit_here = (chip >> jnp.where(core == 0, orders[0][k], orders[1][k])) & 1
        partner = [(j, j ^ (2 << orders[j % 2][k])) for j in range(n)]
        got = lax.ppermute(cur, axis, partner)
        if k == bits - 1:
            got, companion = lax.optimization_barrier((got, companion))
        if k == 0:
            before = work(cur.reshape(-1, width))
        cur = _interleave(cur, got, bit_here)
    if bits:
        cur, before = lax.optimization_barrier((cur, before))
        after = work(got.reshape(-1, width))
    other = lax.ppermute(cur, axis, [(j, j ^ 1) for j in range(n)])
    if not bits:
        return work(block), other.reshape(-1, width), companion
    other, after = lax.optimization_barrier((other, after))
    shaped = lambda r: r.reshape(got.shape[0], block.shape[0], *r.shape[1:])
    done = [_interleave(shaped(b), shaped(a), bit_here) for b, a in zip(before, after)]
    return [d.reshape(-1, *d.shape[2:]) for d in done], other.reshape(-1, width), companion


def halving_rest(keep, send, axis, chains=2):
    n = lax.axis_size(axis)
    chips = n // 2
    bits = chips.bit_length() - 1
    me = lax.axis_index(axis)
    core, chip = me % 2, me // 2
    got = lax.ppermute(send, axis, [(j, j ^ 1) for j in range(n)])
    total = (keep + got.astype(jnp.float32)).reshape(chips, -1, keep.shape[-1])
    orders = _orders(bits)
    outs = []
    for number, cur in enumerate(jnp.split(total, chains, axis=2)):
        sequence = [_swap01(t, bits) if number % 2 else t for t in range(bits)]
        cur = cur.reshape([2] * bits + list(cur.shape[1:]))
        axes = [bits - 1 - a for a in range(bits)]
        for position in sequence:
            at = axes.index(position)
            bit_here = (chip >> jnp.where(core == 0, orders[0][position], orders[1][position])) & 1
            kept = lax.dynamic_index_in_dim(cur, bit_here, axis=at, keepdims=False)
            sent = lax.dynamic_index_in_dim(cur, 1 - bit_here, axis=at, keepdims=False)
            partner = [(j, j ^ (2 << orders[j % 2][position])) for j in range(n)]
            got = lax.ppermute(sent.astype(jnp.bfloat16), axis, partner)
            cur = kept + got.astype(jnp.float32)
            axes.pop(at)
        outs.append(cur)
    return jnp.concatenate(outs, axis=1)


def expert_hidden(packed, w_gate, w_up, model_width, experts, expert):
    rows = packed[:, :model_width]
    parts = packed[:, model_width:model_width + 3 * experts].astype(jnp.float32)
    parts = parts.reshape(-1, 3, experts)
    weight_all = parts[:, 0] + (parts[:, 1] + parts[:, 2])
    weight = jnp.sum(jnp.where(jnp.arange(experts)[None, :] == expert, weight_all, 0.0), axis=1)
    gate_act = jnp.dot(rows, w_gate, preferred_element_type=jnp.float32)
    up_act = jnp.dot(rows, w_up, preferred_element_type=jnp.float32)
    hidden = (jax.nn.silu(gate_act) * up_act).astype(jnp.bfloat16)
    return hidden, weight


def shards(moe_rows, routes, route_weights, w_gate, w_up, w_down, queries, latent_cache, lengths):
    attn_out = attend(queries, latent_cache, lengths)
    rows_here, model_width = moe_rows.shape
    experts = lax.axis_size("ep") // 2
    expert = lax.axis_index("ep") // 2
    named = routes[:, :, None] == jnp.arange(experts, dtype=jnp.int32)[None, None, :]
    dense_w = jnp.sum(jnp.where(named, route_weights[:, :, None], 0.0), axis=1)
    hi = lax.reduce_precision(dense_w, exponent_bits=8, mantissa_bits=7)
    rest = dense_w - hi
    mid = lax.reduce_precision(rest, exponent_bits=8, mantissa_bits=7)
    lo = rest - mid
    hi, mid, lo = (p.astype(jnp.bfloat16) for p in (hi, mid, lo))
    extra = -(-3 * experts // 128) * 128
    tail = jnp.zeros((rows_here, extra - 3 * experts), jnp.bfloat16)
    packed = jnp.concatenate([moe_rows, hi, mid, lo, tail], axis=1)
    args = (w_gate[0], w_up[0], model_width, experts, expert)
    (keep_hidden, keep_weight), other, attn_out = doubling_gather(
        packed, "ep", lambda rows: expert_hidden(rows, *args), attn_out
    )
    send_hidden, send_weight = expert_hidden(other, *args)
    send = jnp.dot(send_hidden, w_down[0], preferred_element_type=jnp.float32)
    send = (send * send_weight[:, None]).astype(jnp.bfloat16)
    keep = jnp.dot(keep_hidden, w_down[0], preferred_element_type=jnp.float32)
    keep = lax.optimization_barrier(keep * keep_weight[:, None])
    moe_out = halving_rest(keep, send, "ep")
    return (moe_out.astype(jnp.bfloat16), attn_out)


def solution(mesh):
    in_specs = (
        P(("dp", "ep"), None),
        P(("dp", "ep"), None),
        P(("dp", "ep"), None),
        P("ep", None, None),
        P("ep", None, None),
        P("ep", None, None),
        P(("dp", "ep"), None, None),
        P(("dp", "ep"), None, None),
        P(("dp", "ep")),
    )
    out_specs = (P(("dp", "ep"), None), P(("dp", "ep"), None, None))
    return jax.shard_map(shards, mesh=mesh, in_specs=in_specs, out_specs=out_specs, check_vma=False)
```

```python
import jax
import jax.numpy as jnp
from jax import lax
from jax.sharding import PartitionSpec as P

LATENT = 512


score_scale = 192.0 ** (-0.5)


def attend(queries, latent_cache, lengths):
    scores = (
        jnp.einsum("rhc,rlc->rhl", queries, latent_cache, preferred_element_type=jnp.float32)
        * score_scale
    )
    in_range = (
        jnp.arange(latent_cache.shape[1], dtype=jnp.int32)[None, None, :] < lengths[:, None, None]
    )
    scores = jnp.where(in_range, scores, -1e30)
    highest = jnp.max(scores, axis=-1, keepdims=True)
    expo = jnp.where(in_range, jnp.exp(scores - highest), 0.0)
    probs = (expo / jnp.sum(expo, axis=-1, keepdims=True)).astype(jnp.bfloat16)
    return jnp.einsum(
        "rhl,rlc->rhc", probs, latent_cache[:, :, :LATENT], preferred_element_type=jnp.float32
    ).astype(jnp.bfloat16)


def _swap01(t, bits):
    return {0: 1, 1: 0}.get(t, t) if bits > 1 else t


def _orders(bits):
    return [list(range(bits)), [_swap01(t, bits) for t in range(bits)]]


def _interleave(a, b, bit):
    pair = jnp.where(bit == 0, jnp.stack([a, b], axis=1), jnp.stack([b, a], axis=1))
    return pair.reshape(2 * a.shape[0], *a.shape[1:])


def doubling_gather(block, axis, work, companion):
    n = lax.axis_size(axis)
    chips = n // 2
    bits = chips.bit_length() - 1
    me = lax.axis_index(axis)
    core, chip = me % 2, me // 2
    orders = _orders(bits)
    width = block.shape[1]
    cur = block[None]
    for k in reversed(range(bits)):
        bit_here = (chip >> jnp.where(core == 0, orders[0][k], orders[1][k])) & 1
        partner = [(j, j ^ (2 << orders[j % 2][k])) for j in range(n)]
        got = lax.ppermute(cur, axis, partner)
        if k == bits - 1:
            got, companion = lax.optimization_barrier((got, companion))
        if k == 0:
            before = work(cur.reshape(-1, width))
        cur = _interleave(cur, got, bit_here)
    if bits:
        cur, before = lax.optimization_barrier((cur, before))
        after = work(got.reshape(-1, width))
    other = lax.ppermute(cur, axis, [(j, j ^ 1) for j in range(n)])
    if not bits:
        return work(block), other.reshape(-1, width), companion
    other, after = lax.optimization_barrier((other, after))
    shaped = lambda r: r.reshape(got.shape[0], block.shape[0], *r.shape[1:])
    done = [_interleave(shaped(b), shaped(a), bit_here) for b, a in zip(before, after)]
    return [d.reshape(-1, *d.shape[2:]) for d in done], other.reshape(-1, width), companion


def halving_rest(keep, send, axis, chains=2):
    n = lax.axis_size(axis)
    chips = n // 2
    bits = chips.bit_length() - 1
    me = lax.axis_index(axis)
    core, chip = me % 2, me // 2
    first = lax.ppermute(send, axis, [(j, j ^ 1) for j in range(n)])
    width = keep.shape[-1] // chains
    outs = []
    for number in range(chains):
        columns = slice(number * width, (number + 1) * width)
        cur = (keep[:, columns] + first[:, columns].astype(jnp.float32)).reshape(chips, -1, width)
        for t in range(bits):
            order = jnp.where(core == 0, t, _swap01(t, bits))
            bit_here = (chip >> order) & 1
            pairs = cur.reshape(cur.shape[0] // 2, 2, *cur.shape[1:])
            kept = lax.dynamic_index_in_dim(pairs, bit_here, axis=1, keepdims=False)
            sent = lax.dynamic_index_in_dim(pairs, 1 - bit_here, axis=1, keepdims=False)
            partner = [(j, j ^ (2 << (t if j % 2 == 0 else _swap01(t, bits)))) for j in range(n)]
            got = lax.ppermute(sent.astype(jnp.bfloat16), axis, partner)
            cur = kept + got.astype(jnp.float32)
        outs.append(cur[0])
    return jnp.concatenate(outs, axis=1)


def expert_hidden(packed, w_gate, w_up, model_width, experts, expert):
    rows = packed[:, :model_width]
    parts = packed[:, model_width:model_width + 3 * experts].astype(jnp.float32)
    parts = parts.reshape(-1, 3, experts)
    weight_all = parts[:, 0] + (parts[:, 1] + parts[:, 2])
    weight = jnp.sum(jnp.where(jnp.arange(experts)[None, :] == expert, weight_all, 0.0), axis=1)
    gate_act = jnp.dot(rows, w_gate, preferred_element_type=jnp.float32)
    up_act = jnp.dot(rows, w_up, preferred_element_type=jnp.float32)
    hidden = (jax.nn.silu(gate_act) * up_act).astype(jnp.bfloat16)
    return hidden, weight


def shards(moe_rows, routes, route_weights, w_gate, w_up, w_down, queries, latent_cache, lengths):
    attn_out = attend(queries, latent_cache, lengths)
    rows_here, model_width = moe_rows.shape
    experts = lax.axis_size("ep") // 2
    expert = lax.axis_index("ep") // 2
    named = routes[:, :, None] == jnp.arange(experts, dtype=jnp.int32)[None, None, :]
    dense_w = jnp.sum(jnp.where(named, route_weights[:, :, None], 0.0), axis=1)
    hi = lax.reduce_precision(dense_w, exponent_bits=8, mantissa_bits=7)
    rest = dense_w - hi
    mid = lax.reduce_precision(rest, exponent_bits=8, mantissa_bits=7)
    lo = rest - mid
    hi, mid, lo = (p.astype(jnp.bfloat16) for p in (hi, mid, lo))
    extra = -(-3 * experts // 128) * 128
    tail = jnp.zeros((rows_here, extra - 3 * experts), jnp.bfloat16)
    packed = jnp.concatenate([moe_rows, hi, mid, lo, tail], axis=1)
    args = (w_gate[0], w_up[0], model_width, experts, expert)
    (keep_hidden, keep_weight), other, attn_out = doubling_gather(
        packed, "ep", lambda rows: expert_hidden(rows, *args), attn_out
    )
    send_hidden, send_weight = expert_hidden(other, *args)
    send = jnp.dot(send_hidden, w_down[0], preferred_element_type=jnp.float32)
    send = (send * send_weight[:, None]).astype(jnp.bfloat16)
    keep = jnp.dot(keep_hidden, w_down[0], preferred_element_type=jnp.float32)
    keep = lax.optimization_barrier(keep * keep_weight[:, None])
    moe_out = halving_rest(keep, send, "ep")
    return (moe_out.astype(jnp.bfloat16), attn_out)


def solution(mesh):
    in_specs = (
        P(("dp", "ep"), None),
        P(("dp", "ep"), None),
        P(("dp", "ep"), None),
        P("ep", None, None),
        P("ep", None, None),
        P("ep", None, None),
        P(("dp", "ep"), None, None),
        P(("dp", "ep"), None, None),
        P(("dp", "ep")),
    )
    out_specs = (P(("dp", "ep"), None), P(("dp", "ep"), None, None))
    return jax.shard_map(shards, mesh=mesh, in_specs=in_specs, out_specs=out_specs, check_vma=False)
```

```python
import jax
import jax.numpy as jnp
from jax import lax
from jax.sharding import PartitionSpec as P

LATENT = 512


score_scale = 192.0 ** (-0.5)


def attend(queries, latent_cache, lengths):
    scores = (
        jnp.einsum("rhc,rlc->rhl", queries, latent_cache, preferred_element_type=jnp.float32)
        * score_scale
    )
    in_range = (
        jnp.arange(latent_cache.shape[1], dtype=jnp.int32)[None, None, :] < lengths[:, None, None]
    )
    scores = jnp.where(in_range, scores, -1e30)
    highest = jnp.max(scores, axis=-1, keepdims=True)
    expo = jnp.where(in_range, jnp.exp(scores - highest), 0.0)
    probs = (expo / jnp.sum(expo, axis=-1, keepdims=True)).astype(jnp.bfloat16)
    return jnp.einsum(
        "rhl,rlc->rhc", probs, latent_cache[:, :, :LATENT], preferred_element_type=jnp.float32
    ).astype(jnp.bfloat16)


def _swap01(t, bits):
    return {0: 1, 1: 0}.get(t, t) if bits > 1 else t


def _orders(bits):
    return [list(range(bits)), [_swap01(t, bits) for t in range(bits)]]


def _interleave(a, b, bit):
    pair = jnp.where(bit == 0, jnp.stack([a, b], axis=1), jnp.stack([b, a], axis=1))
    return pair.reshape(2 * a.shape[0], *a.shape[1:])


def doubling_gather(block, axis, work, companion):
    n = lax.axis_size(axis)
    chips = n // 2
    bits = chips.bit_length() - 1
    me = lax.axis_index(axis)
    core, chip = me % 2, me // 2
    orders = _orders(bits)
    width = block.shape[1]
    cut = width // 2 // 128 * 128
    curs = [block[None, :, :cut], block[None, :, cut:]]
    last = [None, None]
    steps = list(reversed(range(bits)))
    for i in range(bits + 1):
        for c, at in ((0, i), (1, i - 1)):
            if not 0 <= at < bits:
                continue
            k = steps[at]
            bit_here = (chip >> jnp.where(core == 0, orders[0][k], orders[1][k])) & 1
            partner = [(j, j ^ (2 << orders[j % 2][k])) for j in range(n)]
            got = lax.ppermute(curs[c], axis, partner)
            if c == 0 and at == 0:
                got, companion, curs[1] = lax.optimization_barrier((got, companion, curs[1]))
            if k == 0:
                last[c] = (curs[c], got)
            curs[c] = _interleave(curs[c], got, bit_here)
    join = lambda a, b: jnp.concatenate([a, b], axis=-1)
    before = work(join(last[0][0], last[1][0]).reshape(-1, width))
    got = join(last[0][1], last[1][1])
    cur = join(curs[0], curs[1])
    if bits:
        cur, before = lax.optimization_barrier((cur, before))
        after = work(got.reshape(-1, width))
    other = lax.ppermute(cur, axis, [(j, j ^ 1) for j in range(n)])
    if not bits:
        return work(block), other.reshape(-1, width), companion
    other, after = lax.optimization_barrier((other, after))
    shaped = lambda r: r.reshape(got.shape[0], block.shape[0], *r.shape[1:])
    done = [_interleave(shaped(b), shaped(a), bit_here) for b, a in zip(before, after)]
    return [d.reshape(-1, *d.shape[2:]) for d in done], other.reshape(-1, width), companion


def halving_rest(keep, send, axis, chains=2):
    n = lax.axis_size(axis)
    chips = n // 2
    bits = chips.bit_length() - 1
    me = lax.axis_index(axis)
    core, chip = me % 2, me // 2
    got = lax.ppermute(send, axis, [(j, j ^ 1) for j in range(n)])
    total = (keep + got.astype(jnp.float32)).reshape(chips, -1, keep.shape[-1])
    outs = []
    for cur in jnp.split(total, chains, axis=2):
        for t in range(bits):
            order = jnp.where(core == 0, t, _swap01(t, bits))
            bit_here = (chip >> order) & 1
            pairs = cur.reshape(cur.shape[0] // 2, 2, *cur.shape[1:])
            kept = lax.dynamic_index_in_dim(pairs, bit_here, axis=1, keepdims=False)
            sent = lax.dynamic_index_in_dim(pairs, 1 - bit_here, axis=1, keepdims=False)
            partner = [(j, j ^ (2 << (t if j % 2 == 0 else _swap01(t, bits)))) for j in range(n)]
            got = lax.ppermute(sent.astype(jnp.bfloat16), axis, partner)
            cur = kept + got.astype(jnp.float32)
        outs.append(cur[0])
    return jnp.concatenate(outs, axis=1)


def expert_hidden(packed, w_gate, w_up, model_width, experts, expert):
    rows = packed[:, :model_width]
    parts = packed[:, model_width:model_width + 3 * experts].astype(jnp.float32)
    parts = parts.reshape(-1, 3, experts)
    weight_all = parts[:, 0] + (parts[:, 1] + parts[:, 2])
    weight = jnp.sum(jnp.where(jnp.arange(experts)[None, :] == expert, weight_all, 0.0), axis=1)
    gate_act = jnp.dot(rows, w_gate, preferred_element_type=jnp.float32)
    up_act = jnp.dot(rows, w_up, preferred_element_type=jnp.float32)
    hidden = (jax.nn.silu(gate_act) * up_act).astype(jnp.bfloat16)
    return hidden, weight


def shards(moe_rows, routes, route_weights, w_gate, w_up, w_down, queries, latent_cache, lengths):
    attn_out = attend(queries, latent_cache, lengths)
    rows_here, model_width = moe_rows.shape
    experts = lax.axis_size("ep") // 2
    expert = lax.axis_index("ep") // 2
    named = routes[:, :, None] == jnp.arange(experts, dtype=jnp.int32)[None, None, :]
    dense_w = jnp.sum(jnp.where(named, route_weights[:, :, None], 0.0), axis=1)
    hi = lax.reduce_precision(dense_w, exponent_bits=8, mantissa_bits=7)
    rest = dense_w - hi
    mid = lax.reduce_precision(rest, exponent_bits=8, mantissa_bits=7)
    lo = rest - mid
    hi, mid, lo = (p.astype(jnp.bfloat16) for p in (hi, mid, lo))
    extra = -(-3 * experts // 128) * 128
    tail = jnp.zeros((rows_here, extra - 3 * experts), jnp.bfloat16)
    packed = jnp.concatenate([moe_rows, hi, mid, lo, tail], axis=1)
    args = (w_gate[0], w_up[0], model_width, experts, expert)
    (keep_hidden, keep_weight), other, attn_out = doubling_gather(
        packed, "ep", lambda rows: expert_hidden(rows, *args), attn_out
    )
    send_hidden, send_weight = expert_hidden(other, *args)
    send = jnp.dot(send_hidden, w_down[0], preferred_element_type=jnp.float32)
    send = (send * send_weight[:, None]).astype(jnp.bfloat16)
    keep = jnp.dot(keep_hidden, w_down[0], preferred_element_type=jnp.float32)
    keep = lax.optimization_barrier(keep * keep_weight[:, None])
    moe_out = halving_rest(keep, send, "ep")
    return (moe_out.astype(jnp.bfloat16), attn_out)


def solution(mesh):
    in_specs = (
        P(("dp", "ep"), None),
        P(("dp", "ep"), None),
        P(("dp", "ep"), None),
        P("ep", None, None),
        P("ep", None, None),
        P("ep", None, None),
        P(("dp", "ep"), None, None),
        P(("dp", "ep"), None, None),
        P(("dp", "ep")),
    )
    out_specs = (P(("dp", "ep"), None), P(("dp", "ep"), None, None))
    return jax.shard_map(shards, mesh=mesh, in_specs=in_specs, out_specs=out_specs, check_vma=False)
```

```python
import jax
import jax.numpy as jnp
from jax import lax
from jax.sharding import PartitionSpec as P

LATENT = 512


score_scale = 192.0 ** (-0.5)


def attend(queries, latent_cache, lengths):
    scores = (
        jnp.einsum("rhc,rlc->rhl", queries, latent_cache, preferred_element_type=jnp.float32)
        * score_scale
    )
    in_range = (
        jnp.arange(latent_cache.shape[1], dtype=jnp.int32)[None, None, :] < lengths[:, None, None]
    )
    scores = jnp.where(in_range, scores, -1e30)
    highest = jnp.max(scores, axis=-1, keepdims=True)
    expo = jnp.where(in_range, jnp.exp(scores - highest), 0.0)
    probs = (expo / jnp.sum(expo, axis=-1, keepdims=True)).astype(jnp.bfloat16)
    return jnp.einsum(
        "rhl,rlc->rhc", probs, latent_cache[:, :, :LATENT], preferred_element_type=jnp.float32
    ).astype(jnp.bfloat16)


def _swap01(t, bits):
    return {0: 1, 1: 0}.get(t, t) if bits > 1 else t


def _orders(bits):
    return [list(range(bits)), [_swap01(t, bits) for t in range(bits)]]


def _interleave(a, b, bit):
    pair = jnp.where(bit == 0, jnp.stack([a, b], axis=1), jnp.stack([b, a], axis=1))
    return pair.reshape(2 * a.shape[0], *a.shape[1:])


def doubling_gather(block, axis, work, companion):
    n = lax.axis_size(axis)
    chips = n // 2
    bits = chips.bit_length() - 1
    me = lax.axis_index(axis)
    core, chip = me % 2, me // 2
    orders = _orders(bits)
    width = block.shape[1]
    cur = block[None]
    for k in reversed(range(bits)):
        bit_here = (chip >> jnp.where(core == 0, orders[0][k], orders[1][k])) & 1
        partner = [(j, j ^ (2 << orders[j % 2][k])) for j in range(n)]
        got = lax.ppermute(cur, axis, partner)
        if k == bits - 1:
            got, companion = lax.optimization_barrier((got, companion))
        if k == 0:
            before = work(cur.reshape(-1, width))
        cur = _interleave(cur, got, bit_here)
    if bits:
        cur, before = lax.optimization_barrier((cur, before))
        after = work(got.reshape(-1, width))
    other = lax.ppermute(cur, axis, [(j, j ^ 1) for j in range(n)])
    if not bits:
        return work(block), other.reshape(-1, width), companion
    other, after = lax.optimization_barrier((other, after))
    shaped = lambda r: r.reshape(got.shape[0], block.shape[0], *r.shape[1:])
    done = [_interleave(shaped(b), shaped(a), bit_here) for b, a in zip(before, after)]
    return [d.reshape(-1, *d.shape[2:]) for d in done], other.reshape(-1, width), companion


def halving_rest(keep, send, axis, chains=1):
    n = lax.axis_size(axis)
    chips = n // 2
    bits = chips.bit_length() - 1
    me = lax.axis_index(axis)
    core, chip = me % 2, me // 2
    got = lax.ppermute(send, axis, [(j, j ^ 1) for j in range(n)])
    total = (keep + got.astype(jnp.float32)).reshape(chips, -1, keep.shape[-1])
    outs = []
    for cur in jnp.split(total, chains, axis=2):
        for t in range(bits):
            order = jnp.where(core == 0, t, _swap01(t, bits))
            bit_here = (chip >> order) & 1
            pairs = cur.reshape(cur.shape[0] // 2, 2, *cur.shape[1:])
            kept = lax.dynamic_index_in_dim(pairs, bit_here, axis=1, keepdims=False)
            sent = lax.dynamic_index_in_dim(pairs, 1 - bit_here, axis=1, keepdims=False)
            partner = [(j, j ^ (2 << (t if j % 2 == 0 else _swap01(t, bits)))) for j in range(n)]
            got = lax.ppermute(sent.astype(jnp.bfloat16), axis, partner)
            cur = kept + got.astype(jnp.float32)
        outs.append(cur[0])
    return jnp.concatenate(outs, axis=1)


def expert_hidden(packed, w_gate, w_up, model_width, experts, expert):
    rows = packed[:, :model_width]
    parts = packed[:, model_width:model_width + 3 * experts].astype(jnp.float32)
    parts = parts.reshape(-1, 3, experts)
    weight_all = parts[:, 0] + (parts[:, 1] + parts[:, 2])
    weight = jnp.sum(jnp.where(jnp.arange(experts)[None, :] == expert, weight_all, 0.0), axis=1)
    gate_act = jnp.dot(rows, w_gate, preferred_element_type=jnp.float32)
    up_act = jnp.dot(rows, w_up, preferred_element_type=jnp.float32)
    hidden = (jax.nn.silu(gate_act) * up_act).astype(jnp.bfloat16)
    return hidden, weight


def shards(moe_rows, routes, route_weights, w_gate, w_up, w_down, queries, latent_cache, lengths):
    attn_out = attend(queries, latent_cache, lengths)
    rows_here, model_width = moe_rows.shape
    experts = lax.axis_size("ep") // 2
    expert = lax.axis_index("ep") // 2
    named = routes[:, :, None] == jnp.arange(experts, dtype=jnp.int32)[None, None, :]
    dense_w = jnp.sum(jnp.where(named, route_weights[:, :, None], 0.0), axis=1)
    hi = lax.reduce_precision(dense_w, exponent_bits=8, mantissa_bits=7)
    rest = dense_w - hi
    mid = lax.reduce_precision(rest, exponent_bits=8, mantissa_bits=7)
    lo = rest - mid
    hi, mid, lo = (p.astype(jnp.bfloat16) for p in (hi, mid, lo))
    extra = -(-3 * experts // 128) * 128
    tail = jnp.zeros((rows_here, extra - 3 * experts), jnp.bfloat16)
    packed = jnp.concatenate([moe_rows, hi, mid, lo, tail], axis=1)
    args = (w_gate[0], w_up[0], model_width, experts, expert)
    (keep_hidden, keep_weight), other, attn_out = doubling_gather(
        packed, "ep", lambda rows: expert_hidden(rows, *args), attn_out
    )
    send_hidden, send_weight = expert_hidden(other, *args)
    send = jnp.dot(send_hidden, w_down[0], preferred_element_type=jnp.float32)
    send = (send * send_weight[:, None]).astype(jnp.bfloat16)
    keep = jnp.dot(keep_hidden, w_down[0], preferred_element_type=jnp.float32)
    keep = lax.optimization_barrier(keep * keep_weight[:, None])
    moe_out = halving_rest(keep, send, "ep")
    return (moe_out.astype(jnp.bfloat16), attn_out)


def solution(mesh):
    in_specs = (
        P(("dp", "ep"), None),
        P(("dp", "ep"), None),
        P(("dp", "ep"), None),
        P("ep", None, None),
        P("ep", None, None),
        P("ep", None, None),
        P(("dp", "ep"), None, None),
        P(("dp", "ep"), None, None),
        P(("dp", "ep")),
    )
    out_specs = (P(("dp", "ep"), None), P(("dp", "ep"), None, None))
    return jax.shard_map(shards, mesh=mesh, in_specs=in_specs, out_specs=out_specs, check_vma=False)
```

```python
import jax
import jax.numpy as jnp
from jax import lax
from jax.sharding import PartitionSpec as P

LATENT = 512


score_scale = 192.0 ** (-0.5)


def attend(queries, latent_cache, lengths):
    scores = (
        jnp.einsum("rhc,rlc->rhl", queries, latent_cache, preferred_element_type=jnp.float32)
        * score_scale
    )
    in_range = (
        jnp.arange(latent_cache.shape[1], dtype=jnp.int32)[None, None, :] < lengths[:, None, None]
    )
    scores = jnp.where(in_range, scores, -1e30)
    highest = jnp.max(scores, axis=-1, keepdims=True)
    expo = jnp.where(in_range, jnp.exp(scores - highest), 0.0)
    probs = (expo / jnp.sum(expo, axis=-1, keepdims=True)).astype(jnp.bfloat16)
    return jnp.einsum(
        "rhl,rlc->rhc", probs, latent_cache[:, :, :LATENT], preferred_element_type=jnp.float32
    ).astype(jnp.bfloat16)


def _swap01(t, bits):
    return {0: 1, 1: 0}.get(t, t) if bits > 1 else t


def _orders(bits):
    return [list(range(bits)), [_swap01(t, bits) for t in range(bits)]]


def _interleave(a, b, bit):
    pair = jnp.where(bit == 0, jnp.stack([a, b], axis=1), jnp.stack([b, a], axis=1))
    return pair.reshape(2 * a.shape[0], *a.shape[1:])


def doubling_gather(block, axis, work, companion):
    n = lax.axis_size(axis)
    chips = n // 2
    bits = chips.bit_length() - 1
    me = lax.axis_index(axis)
    core, chip = me % 2, me // 2
    orders = _orders(bits)
    width = block.shape[1]
    cur = block[None]
    for k in reversed(range(bits)):
        bit_here = (chip >> jnp.where(core == 0, orders[0][k], orders[1][k])) & 1
        partner = [(j, j ^ (2 << orders[j % 2][k])) for j in range(n)]
        got = lax.ppermute(cur, axis, partner)
        if k == bits - 1:
            got, companion = lax.optimization_barrier((got, companion))
        if k == 0:
            before = work(cur.reshape(-1, width))
        cur = _interleave(cur, got, bit_here)
    if bits:
        cur, before = lax.optimization_barrier((cur, before))
        after = work(got.reshape(-1, width))
    other = lax.ppermute(cur, axis, [(j, j ^ 1) for j in range(n)])
    if not bits:
        return work(block), other.reshape(-1, width), companion
    other, after = lax.optimization_barrier((other, after))
    shaped = lambda r: r.reshape(got.shape[0], block.shape[0], *r.shape[1:])
    done = [_interleave(shaped(b), shaped(a), bit_here) for b, a in zip(before, after)]
    return [d.reshape(-1, *d.shape[2:]) for d in done], other.reshape(-1, width), companion


def halving_rest(keep, send, axis, chains=2):
    n = lax.axis_size(axis)
    chips = n // 2
    bits = chips.bit_length() - 1
    me = lax.axis_index(axis)
    core, chip = me % 2, me // 2
    got = lax.ppermute(send, axis, [(j, j ^ 1) for j in range(n)])
    total = (keep + got.astype(jnp.float32)).reshape(chips, -1, keep.shape[-1])
    outs = []
    lead = None
    for cur in jnp.split(total, chains, axis=2):
        for t in range(bits):
            order = jnp.where(core == 0, t, _swap01(t, bits))
            bit_here = (chip >> order) & 1
            pairs = cur.reshape(cur.shape[0] // 2, 2, *cur.shape[1:])
            kept = lax.dynamic_index_in_dim(pairs, bit_here, axis=1, keepdims=False)
            sent = lax.dynamic_index_in_dim(pairs, 1 - bit_here, axis=1, keepdims=False)
            if t == 0 and lead is not None:
                sent, lead = lax.optimization_barrier((sent, lead))
            partner = [(j, j ^ (2 << (t if j % 2 == 0 else _swap01(t, bits)))) for j in range(n)]
            got = lax.ppermute(sent.astype(jnp.bfloat16), axis, partner)
            if t == 0:
                lead = got
            cur = kept + got.astype(jnp.float32)
        outs.append(cur[0])
    return jnp.concatenate(outs, axis=1)


def expert_hidden(packed, w_gate, w_up, model_width, experts, expert):
    rows = packed[:, :model_width]
    parts = packed[:, model_width:model_width + 3 * experts].astype(jnp.float32)
    parts = parts.reshape(-1, 3, experts)
    weight_all = parts[:, 0] + (parts[:, 1] + parts[:, 2])
    weight = jnp.sum(jnp.where(jnp.arange(experts)[None, :] == expert, weight_all, 0.0), axis=1)
    gate_act = jnp.dot(rows, w_gate, preferred_element_type=jnp.float32)
    up_act = jnp.dot(rows, w_up, preferred_element_type=jnp.float32)
    hidden = (jax.nn.silu(gate_act) * up_act).astype(jnp.bfloat16)
    return hidden, weight


def shards(moe_rows, routes, route_weights, w_gate, w_up, w_down, queries, latent_cache, lengths):
    attn_out = attend(queries, latent_cache, lengths)
    rows_here, model_width = moe_rows.shape
    experts = lax.axis_size("ep") // 2
    expert = lax.axis_index("ep") // 2
    named = routes[:, :, None] == jnp.arange(experts, dtype=jnp.int32)[None, None, :]
    dense_w = jnp.sum(jnp.where(named, route_weights[:, :, None], 0.0), axis=1)
    hi = lax.reduce_precision(dense_w, exponent_bits=8, mantissa_bits=7)
    rest = dense_w - hi
    mid = lax.reduce_precision(rest, exponent_bits=8, mantissa_bits=7)
    lo = rest - mid
    hi, mid, lo = (p.astype(jnp.bfloat16) for p in (hi, mid, lo))
    extra = -(-3 * experts // 128) * 128
    tail = jnp.zeros((rows_here, extra - 3 * experts), jnp.bfloat16)
    packed = jnp.concatenate([moe_rows, hi, mid, lo, tail], axis=1)
    args = (w_gate[0], w_up[0], model_width, experts, expert)
    (keep_hidden, keep_weight), other, attn_out = doubling_gather(
        packed, "ep", lambda rows: expert_hidden(rows, *args), attn_out
    )
    send_hidden, send_weight = expert_hidden(other, *args)
    send = jnp.dot(send_hidden, w_down[0], preferred_element_type=jnp.float32)
    send = (send * send_weight[:, None]).astype(jnp.bfloat16)
    keep = jnp.dot(keep_hidden, w_down[0], preferred_element_type=jnp.float32)
    keep = lax.optimization_barrier(keep * keep_weight[:, None])
    moe_out = halving_rest(keep, send, "ep")
    return (moe_out.astype(jnp.bfloat16), attn_out)


def solution(mesh):
    in_specs = (
        P(("dp", "ep"), None),
        P(("dp", "ep"), None),
        P(("dp", "ep"), None),
        P("ep", None, None),
        P("ep", None, None),
        P("ep", None, None),
        P(("dp", "ep"), None, None),
        P(("dp", "ep"), None, None),
        P(("dp", "ep")),
    )
    out_specs = (P(("dp", "ep"), None), P(("dp", "ep"), None, None))
    return jax.shard_map(shards, mesh=mesh, in_specs=in_specs, out_specs=out_specs, check_vma=False)
```

```python
import jax
import jax.numpy as jnp
from jax import lax
from jax.sharding import PartitionSpec as P

LATENT = 512


score_scale = 192.0 ** (-0.5)


def attend(queries, latent_cache, lengths):
    scores = (
        jnp.einsum("rhc,rlc->rhl", queries, latent_cache, preferred_element_type=jnp.float32)
        * score_scale
    )
    in_range = (
        jnp.arange(latent_cache.shape[1], dtype=jnp.int32)[None, None, :] < lengths[:, None, None]
    )
    scores = jnp.where(in_range, scores, -1e30)
    highest = jnp.max(scores, axis=-1, keepdims=True)
    expo = jnp.where(in_range, jnp.exp(scores - highest), 0.0)
    probs = (expo / jnp.sum(expo, axis=-1, keepdims=True)).astype(jnp.bfloat16)
    return jnp.einsum(
        "rhl,rlc->rhc", probs, latent_cache[:, :, :LATENT], preferred_element_type=jnp.float32
    ).astype(jnp.bfloat16)


def _swap01(t, bits):
    return {0: 1, 1: 0}.get(t, t) if bits > 1 else t


def _orders(bits):
    return [list(range(bits)), [_swap01(t, bits) for t in range(bits)]]


def _interleave(a, b, bit):
    pair = jnp.where(bit == 0, jnp.stack([a, b], axis=1), jnp.stack([b, a], axis=1))
    return pair.reshape(2 * a.shape[0], *a.shape[1:])


def doubling_gather(block, axis, work, companion):
    n = lax.axis_size(axis)
    chips = n // 2
    bits = chips.bit_length() - 1
    me = lax.axis_index(axis)
    core, chip = me % 2, me // 2
    orders = _orders(bits)
    width = block.shape[1]
    cur = block[None]
    for k in reversed(range(bits)):
        bit_here = (chip >> jnp.where(core == 0, orders[0][k], orders[1][k])) & 1
        partner = [(j, j ^ (2 << orders[j % 2][k])) for j in range(n)]
        got = lax.ppermute(cur, axis, partner)
        if k == bits - 1:
            got, companion = lax.optimization_barrier((got, companion))
        if k == 0:
            before = work(cur.reshape(-1, width))
        cur = _interleave(cur, got, bit_here)
    if bits:
        cur, before = lax.optimization_barrier((cur, before))
        after = work(got.reshape(-1, width))
    other = lax.ppermute(cur, axis, [(j, j ^ 1) for j in range(n)])
    if not bits:
        return work(block), other.reshape(-1, width), companion
    other, after = lax.optimization_barrier((other, after))
    shaped = lambda r: r.reshape(got.shape[0], block.shape[0], *r.shape[1:])
    done = [_interleave(shaped(b), shaped(a), bit_here) for b, a in zip(before, after)]
    return [d.reshape(-1, *d.shape[2:]) for d in done], other.reshape(-1, width), companion


def halving_rest(keep, send, axis, chains=2):
    n = lax.axis_size(axis)
    chips = n // 2
    bits = chips.bit_length() - 1
    me = lax.axis_index(axis)
    core, chip = me % 2, me // 2
    got = lax.ppermute(send, axis, [(j, j ^ 1) for j in range(n)])
    total = (keep + got.astype(jnp.float32)).reshape(chips, -1, keep.shape[-1])
    outs = []
    lead_width = (total.shape[2] // chains // 128 + 3) * 128
    cuts = [lead_width * (c + 1) for c in range(chains - 1)]
    for cur in jnp.split(total, cuts, axis=2):
        for t in range(bits):
            order = jnp.where(core == 0, t, _swap01(t, bits))
            bit_here = (chip >> order) & 1
            pairs = cur.reshape(cur.shape[0] // 2, 2, *cur.shape[1:])
            kept = lax.dynamic_index_in_dim(pairs, bit_here, axis=1, keepdims=False)
            sent = lax.dynamic_index_in_dim(pairs, 1 - bit_here, axis=1, keepdims=False)
            partner = [(j, j ^ (2 << (t if j % 2 == 0 else _swap01(t, bits)))) for j in range(n)]
            got = lax.ppermute(sent.astype(jnp.bfloat16), axis, partner)
            cur = kept + got.astype(jnp.float32)
        outs.append(cur[0])
    return jnp.concatenate(outs, axis=1)


def expert_hidden(packed, w_gate, w_up, model_width, experts, expert):
    rows = packed[:, :model_width]
    parts = packed[:, model_width:model_width + 3 * experts].astype(jnp.float32)
    parts = parts.reshape(-1, 3, experts)
    weight_all = parts[:, 0] + (parts[:, 1] + parts[:, 2])
    weight = jnp.sum(jnp.where(jnp.arange(experts)[None, :] == expert, weight_all, 0.0), axis=1)
    gate_act = jnp.dot(rows, w_gate, preferred_element_type=jnp.float32)
    up_act = jnp.dot(rows, w_up, preferred_element_type=jnp.float32)
    hidden = (jax.nn.silu(gate_act) * up_act).astype(jnp.bfloat16)
    return hidden, weight


def shards(moe_rows, routes, route_weights, w_gate, w_up, w_down, queries, latent_cache, lengths):
    attn_out = attend(queries, latent_cache, lengths)
    rows_here, model_width = moe_rows.shape
    experts = lax.axis_size("ep") // 2
    expert = lax.axis_index("ep") // 2
    named = routes[:, :, None] == jnp.arange(experts, dtype=jnp.int32)[None, None, :]
    dense_w = jnp.sum(jnp.where(named, route_weights[:, :, None], 0.0), axis=1)
    hi = lax.reduce_precision(dense_w, exponent_bits=8, mantissa_bits=7)
    rest = dense_w - hi
    mid = lax.reduce_precision(rest, exponent_bits=8, mantissa_bits=7)
    lo = rest - mid
    hi, mid, lo = (p.astype(jnp.bfloat16) for p in (hi, mid, lo))
    extra = -(-3 * experts // 128) * 128
    tail = jnp.zeros((rows_here, extra - 3 * experts), jnp.bfloat16)
    packed = jnp.concatenate([moe_rows, hi, mid, lo, tail], axis=1)
    args = (w_gate[0], w_up[0], model_width, experts, expert)
    (keep_hidden, keep_weight), other, attn_out = doubling_gather(
        packed, "ep", lambda rows: expert_hidden(rows, *args), attn_out
    )
    send_hidden, send_weight = expert_hidden(other, *args)
    send = jnp.dot(send_hidden, w_down[0], preferred_element_type=jnp.float32)
    send = (send * send_weight[:, None]).astype(jnp.bfloat16)
    keep = jnp.dot(keep_hidden, w_down[0], preferred_element_type=jnp.float32)
    keep = lax.optimization_barrier(keep * keep_weight[:, None])
    moe_out = halving_rest(keep, send, "ep")
    return (moe_out.astype(jnp.bfloat16), attn_out)


def solution(mesh):
    in_specs = (
        P(("dp", "ep"), None),
        P(("dp", "ep"), None),
        P(("dp", "ep"), None),
        P("ep", None, None),
        P("ep", None, None),
        P("ep", None, None),
        P(("dp", "ep"), None, None),
        P(("dp", "ep"), None, None),
        P(("dp", "ep")),
    )
    out_specs = (P(("dp", "ep"), None), P(("dp", "ep"), None, None))
    return jax.shard_map(shards, mesh=mesh, in_specs=in_specs, out_specs=out_specs, check_vma=False)
```

```python
import jax
import jax.numpy as jnp
from jax import lax
from jax.sharding import PartitionSpec as P

LATENT = 512


score_scale = 192.0 ** (-0.5)


def attend(queries, latent_cache, lengths):
    scores = (
        jnp.einsum("rhc,rlc->rhl", queries, latent_cache, preferred_element_type=jnp.float32)
        * score_scale
    )
    in_range = (
        jnp.arange(latent_cache.shape[1], dtype=jnp.int32)[None, None, :] < lengths[:, None, None]
    )
    scores = jnp.where(in_range, scores, -1e30)
    highest = jnp.max(scores, axis=-1, keepdims=True)
    expo = jnp.where(in_range, jnp.exp(scores - highest), 0.0)
    probs = (expo / jnp.sum(expo, axis=-1, keepdims=True)).astype(jnp.bfloat16)
    return jnp.einsum(
        "rhl,rlc->rhc", probs, latent_cache[:, :, :LATENT], preferred_element_type=jnp.float32
    ).astype(jnp.bfloat16)


def _swap01(t, bits):
    return {0: 1, 1: 0}.get(t, t) if bits > 1 else t


def _orders(bits):
    return [list(range(bits)), [_swap01(t, bits) for t in range(bits)]]


def _interleave(a, b, bit):
    pair = jnp.where(bit == 0, jnp.stack([a, b], axis=1), jnp.stack([b, a], axis=1))
    return pair.reshape(2 * a.shape[0], *a.shape[1:])


def doubling_gather(block, axis, work, companion):
    n = lax.axis_size(axis)
    chips = n // 2
    bits = chips.bit_length() - 1
    me = lax.axis_index(axis)
    core, chip = me % 2, me // 2
    orders = _orders(bits)
    width = block.shape[1]
    cur = block[None]
    for k in reversed(range(bits)):
        bit_here = (chip >> jnp.where(core == 0, orders[0][k], orders[1][k])) & 1
        partner = [(j, j ^ (2 << orders[j % 2][k])) for j in range(n)]
        got = lax.ppermute(cur, axis, partner)
        if k == bits - 1:
            got, companion = lax.optimization_barrier((got, companion))
        if k == 0:
            before = work(cur.reshape(-1, width))
        cur = _interleave(cur, got, bit_here)
    if bits:
        cur, before = lax.optimization_barrier((cur, before))
        after = work(got.reshape(-1, width))
    other = lax.ppermute(cur, axis, [(j, j ^ 1) for j in range(n)])
    if not bits:
        return work(block), other.reshape(-1, width), companion
    other, after = lax.optimization_barrier((other, after))
    shaped = lambda r: r.reshape(got.shape[0], block.shape[0], *r.shape[1:])
    done = [_interleave(shaped(b), shaped(a), bit_here) for b, a in zip(before, after)]
    return [d.reshape(-1, *d.shape[2:]) for d in done], other.reshape(-1, width), companion


def halving_rest(keep, send, axis, chains=2):
    n = lax.axis_size(axis)
    chips = n // 2
    bits = chips.bit_length() - 1
    me = lax.axis_index(axis)
    core, chip = me % 2, me // 2
    got = jnp.concatenate([lax.ppermute(p, axis, [(j, j ^ 1) for j in range(n)]) for p in send], axis=0)
    total = (keep + got.astype(jnp.float32)).reshape(chips, -1, keep.shape[-1])
    outs = []
    for cur in jnp.split(total, chains, axis=2):
        for t in range(bits):
            order = jnp.where(core == 0, t, _swap01(t, bits))
            bit_here = (chip >> order) & 1
            pairs = cur.reshape(cur.shape[0] // 2, 2, *cur.shape[1:])
            kept = lax.dynamic_index_in_dim(pairs, bit_here, axis=1, keepdims=False)
            sent = lax.dynamic_index_in_dim(pairs, 1 - bit_here, axis=1, keepdims=False)
            partner = [(j, j ^ (2 << (t if j % 2 == 0 else _swap01(t, bits)))) for j in range(n)]
            got = lax.ppermute(sent.astype(jnp.bfloat16), axis, partner)
            cur = kept + got.astype(jnp.float32)
        outs.append(cur[0])
    return jnp.concatenate(outs, axis=1)


def expert_hidden(packed, w_gate, w_up, model_width, experts, expert):
    rows = packed[:, :model_width]
    parts = packed[:, model_width:model_width + 3 * experts].astype(jnp.float32)
    parts = parts.reshape(-1, 3, experts)
    weight_all = parts[:, 0] + (parts[:, 1] + parts[:, 2])
    weight = jnp.sum(jnp.where(jnp.arange(experts)[None, :] == expert, weight_all, 0.0), axis=1)
    gate_act = jnp.dot(rows, w_gate, preferred_element_type=jnp.float32)
    up_act = jnp.dot(rows, w_up, preferred_element_type=jnp.float32)
    hidden = (jax.nn.silu(gate_act) * up_act).astype(jnp.bfloat16)
    return hidden, weight


def shards(moe_rows, routes, route_weights, w_gate, w_up, w_down, queries, latent_cache, lengths):
    attn_out = attend(queries, latent_cache, lengths)
    rows_here, model_width = moe_rows.shape
    experts = lax.axis_size("ep") // 2
    expert = lax.axis_index("ep") // 2
    named = routes[:, :, None] == jnp.arange(experts, dtype=jnp.int32)[None, None, :]
    dense_w = jnp.sum(jnp.where(named, route_weights[:, :, None], 0.0), axis=1)
    hi = lax.reduce_precision(dense_w, exponent_bits=8, mantissa_bits=7)
    rest = dense_w - hi
    mid = lax.reduce_precision(rest, exponent_bits=8, mantissa_bits=7)
    lo = rest - mid
    hi, mid, lo = (p.astype(jnp.bfloat16) for p in (hi, mid, lo))
    extra = -(-3 * experts // 128) * 128
    tail = jnp.zeros((rows_here, extra - 3 * experts), jnp.bfloat16)
    packed = jnp.concatenate([moe_rows, hi, mid, lo, tail], axis=1)
    args = (w_gate[0], w_up[0], model_width, experts, expert)
    (keep_hidden, keep_weight), other, attn_out = doubling_gather(
        packed, "ep", lambda rows: expert_hidden(rows, *args), attn_out
    )
    def sent_out(rows):
        hidden, weight = expert_hidden(rows, *args)
        out = jnp.dot(hidden, w_down[0], preferred_element_type=jnp.float32)
        return (out * weight[:, None]).astype(jnp.bfloat16)

    send = [sent_out(part) for part in jnp.split(other, 2, axis=0)]
    keep = jnp.dot(keep_hidden, w_down[0], preferred_element_type=jnp.float32)
    keep = lax.optimization_barrier(keep * keep_weight[:, None])
    moe_out = halving_rest(keep, send, "ep")
    return (moe_out.astype(jnp.bfloat16), attn_out)


def solution(mesh):
    in_specs = (
        P(("dp", "ep"), None),
        P(("dp", "ep"), None),
        P(("dp", "ep"), None),
        P("ep", None, None),
        P("ep", None, None),
        P("ep", None, None),
        P(("dp", "ep"), None, None),
        P(("dp", "ep"), None, None),
        P(("dp", "ep")),
    )
    out_specs = (P(("dp", "ep"), None), P(("dp", "ep"), None, None))
    return jax.shard_map(shards, mesh=mesh, in_specs=in_specs, out_specs=out_specs, check_vma=False)
```

```python
import jax
import jax.numpy as jnp
from jax import lax
from jax.sharding import PartitionSpec as P

LATENT = 512


score_scale = 192.0 ** (-0.5)


def attend(queries, latent_cache, lengths):
    scores = (
        jnp.einsum("rhc,rlc->rhl", queries, latent_cache, preferred_element_type=jnp.float32)
        * score_scale
    )
    in_range = (
        jnp.arange(latent_cache.shape[1], dtype=jnp.int32)[None, None, :] < lengths[:, None, None]
    )
    scores = jnp.where(in_range, scores, -1e30)
    highest = jnp.max(scores, axis=-1, keepdims=True)
    expo = jnp.where(in_range, jnp.exp(scores - highest), 0.0)
    probs = (expo / jnp.sum(expo, axis=-1, keepdims=True)).astype(jnp.bfloat16)
    return jnp.einsum(
        "rhl,rlc->rhc", probs, latent_cache[:, :, :LATENT], preferred_element_type=jnp.float32
    ).astype(jnp.bfloat16)


def _swap01(t, bits):
    return {0: 1, 1: 0}.get(t, t) if bits > 1 else t


def _orders(bits):
    return [list(range(bits)), [_swap01(t, bits) for t in range(bits)]]


def _interleave(a, b, bit):
    pair = jnp.where(bit == 0, jnp.stack([a, b], axis=1), jnp.stack([b, a], axis=1))
    return pair.reshape(2 * a.shape[0], *a.shape[1:])


def doubling_gather(block, axis, work, companion):
    n = lax.axis_size(axis)
    chips = n // 2
    bits = chips.bit_length() - 1
    me = lax.axis_index(axis)
    core, chip = me % 2, me // 2
    orders = _orders(bits)
    width = block.shape[1]
    cur = block[None]
    for k in reversed(range(bits)):
        bit_here = (chip >> jnp.where(core == 0, orders[0][k], orders[1][k])) & 1
        partner = [(j, j ^ (2 << orders[j % 2][k])) for j in range(n)]
        got = lax.ppermute(cur, axis, partner)
        if k == bits - 1:
            got, companion = lax.optimization_barrier((got, companion))
        if k == 0:
            before = work(cur.reshape(-1, width))
        cur = _interleave(cur, got, bit_here)
    if bits:
        cur, before = lax.optimization_barrier((cur, before))
        after = work(got.reshape(-1, width))
    other = lax.ppermute(cur, axis, [(j, j ^ 1) for j in range(n)])
    if not bits:
        return work(block), other.reshape(-1, width), companion
    other, after = lax.optimization_barrier((other, after))
    shaped = lambda r: r.reshape(got.shape[0], block.shape[0], *r.shape[1:])
    done = [_interleave(shaped(b), shaped(a), bit_here) for b, a in zip(before, after)]
    return [d.reshape(-1, *d.shape[2:]) for d in done], other.reshape(-1, width), companion


def halving_rest(keep, send, axis, chains=2):
    n = lax.axis_size(axis)
    chips = n // 2
    bits = chips.bit_length() - 1
    me = lax.axis_index(axis)
    core, chip = me % 2, me // 2
    got = lax.ppermute(send, axis, [(j, j ^ 1) for j in range(n)])
    total = (keep + got.astype(jnp.float32)).reshape(chips, -1, keep.shape[-1])
    outs = []
    for cur in jnp.split(total, chains, axis=2):
        for t in range(bits):
            order = jnp.where(core == 0, t, _swap01(t, bits))
            bit_here = (chip >> order) & 1
            pairs = cur.reshape(cur.shape[0] // 2, 2, *cur.shape[1:])
            kept = lax.dynamic_index_in_dim(pairs, bit_here, axis=1, keepdims=False)
            sent = lax.dynamic_index_in_dim(pairs, 1 - bit_here, axis=1, keepdims=False)
            partner = [(j, j ^ (2 << (t if j % 2 == 0 else _swap01(t, bits)))) for j in range(n)]
            got = lax.ppermute(sent.astype(jnp.bfloat16), axis, partner)
            cur = (kept.astype(jnp.float32) + got.astype(jnp.float32)).astype(jnp.bfloat16)
        outs.append(cur[0])
    return jnp.concatenate(outs, axis=1)


def expert_hidden(packed, w_gate, w_up, model_width, experts, expert):
    rows = packed[:, :model_width]
    parts = packed[:, model_width:model_width + 3 * experts].astype(jnp.float32)
    parts = parts.reshape(-1, 3, experts)
    weight_all = parts[:, 0] + (parts[:, 1] + parts[:, 2])
    weight = jnp.sum(jnp.where(jnp.arange(experts)[None, :] == expert, weight_all, 0.0), axis=1)
    gate_act = jnp.dot(rows, w_gate, preferred_element_type=jnp.float32)
    up_act = jnp.dot(rows, w_up, preferred_element_type=jnp.float32)
    hidden = (jax.nn.silu(gate_act) * up_act).astype(jnp.bfloat16)
    return hidden, weight


def shards(moe_rows, routes, route_weights, w_gate, w_up, w_down, queries, latent_cache, lengths):
    attn_out = attend(queries, latent_cache, lengths)
    rows_here, model_width = moe_rows.shape
    experts = lax.axis_size("ep") // 2
    expert = lax.axis_index("ep") // 2
    named = routes[:, :, None] == jnp.arange(experts, dtype=jnp.int32)[None, None, :]
    dense_w = jnp.sum(jnp.where(named, route_weights[:, :, None], 0.0), axis=1)
    hi = lax.reduce_precision(dense_w, exponent_bits=8, mantissa_bits=7)
    rest = dense_w - hi
    mid = lax.reduce_precision(rest, exponent_bits=8, mantissa_bits=7)
    lo = rest - mid
    hi, mid, lo = (p.astype(jnp.bfloat16) for p in (hi, mid, lo))
    extra = -(-3 * experts // 128) * 128
    tail = jnp.zeros((rows_here, extra - 3 * experts), jnp.bfloat16)
    packed = jnp.concatenate([moe_rows, hi, mid, lo, tail], axis=1)
    args = (w_gate[0], w_up[0], model_width, experts, expert)
    (keep_hidden, keep_weight), other, attn_out = doubling_gather(
        packed, "ep", lambda rows: expert_hidden(rows, *args), attn_out
    )
    send_hidden, send_weight = expert_hidden(other, *args)
    send = jnp.dot(send_hidden, w_down[0], preferred_element_type=jnp.float32)
    send = (send * send_weight[:, None]).astype(jnp.bfloat16)
    keep = jnp.dot(keep_hidden, w_down[0], preferred_element_type=jnp.float32)
    keep = lax.optimization_barrier(keep * keep_weight[:, None])
    moe_out = halving_rest(keep, send, "ep")
    return (moe_out.astype(jnp.bfloat16), attn_out)


def solution(mesh):
    in_specs = (
        P(("dp", "ep"), None),
        P(("dp", "ep"), None),
        P(("dp", "ep"), None),
        P("ep", None, None),
        P("ep", None, None),
        P("ep", None, None),
        P(("dp", "ep"), None, None),
        P(("dp", "ep"), None, None),
        P(("dp", "ep")),
    )
    out_specs = (P(("dp", "ep"), None), P(("dp", "ep"), None, None))
    return jax.shard_map(shards, mesh=mesh, in_specs=in_specs, out_specs=out_specs, check_vma=False)
```
